32 devices in a mesh: space: 8 (over z, x), chan: 4 (over y, core).
Axes of the slice: x: 2, y: 2, z: 4, core: 2. Of those that a mesh axis runs over, the one named last changes fastest.
Arguments:
- volume: bfloat16 [8, 4, 64, 512], P('space'), may hold values from -6 to 6
- weight_one: bfloat16 [3, 3, 3, 512, 512], P(None, None, None, 'chan'), may hold values from -0.0546875 to 0.0546875
- bias_one: float32 [512], P('chan'), may hold values from -3 to 3
- weight_two: bfloat16 [3, 3, 3, 512, 512], P(None, None, None, 'chan'), may hold values from -0.0546875 to 0.0546875
- bias_two: float32 [512], P('chan'), may hold values from -3 to 3
Outputs:
- features: bfloat16 [8, 512, 256], P('space', 'chan')
The draws below stay inside these ranges and needn't reach their ends.
All inputs are finite; a program needn't handle non-finite values.
Results may differ from the reference program's by a relative error of at most 0.0044.
Values may be sent and summed in bfloat16 or wider, within the bound.
No kernel may reach another device: no remote copies, remote signals or barrier semaphores. Data moves between devices by JAX's collectives and lax.ppermute only.
A program may use at most 64 MiB of HBM per device.

```python
import jax
import jax.numpy as jnp
from jax import lax

CHANNELS = 512
ROWS = 4
COLS = 64
DEPTH = 8


def steps_of(stream_key, shape, pieces, least, largest):
    level, own = 1.0, jax.random.fold_in(stream_key, 6)
    for axis_at, parts in pieces:
        heights = jnp.exp(jax.random.uniform(jax.random.fold_in(own, axis_at), (parts,), jnp.float32, least / len(pieces), largest / len(pieces)))
        level = level * jnp.repeat(heights, shape[axis_at] // parts).reshape([-1 if axis == axis_at else 1 for axis in range(len(shape))])
    return level


def scatter_about(rng, extent, deviation, limit, split=(), held_as=jnp.bfloat16):
    values = deviation * jax.random.normal(rng, extent, jnp.float32)
    if split:
        values = values * steps_of(rng, extent, split, -0.22, 0.18)
    return jnp.clip(values, -limit, limit).astype(held_as)


def setup_inputs(seed: int = 0) -> dict:
    splits = jax.random.split(jax.random.key(seed), 6)
    volume = scatter_about(splits[0], (DEPTH, ROWS, COLS, CHANNELS), 1.0, 6.0, ((0, 8),))
    weight_one = scatter_about(splits[1], (3, 3, 3, CHANNELS, CHANNELS), (27 * CHANNELS) ** -0.5, 0.0546875, ((3, 4),))
    bias_one = scatter_about(splits[2], (CHANNELS,), 0.5, 3.0, ((0, 4),), jnp.float32)
    weight_two = scatter_about(splits[3], (3, 3, 3, CHANNELS, CHANNELS), (27 * CHANNELS) ** -0.5, 0.0546875, ((3, 4),))
    bias_two = scatter_about(splits[4], (CHANNELS,), 0.5, 3.0, ((0, 4),), jnp.float32)
    return {"volume": volume, "weight_one": weight_one, "bias_one": bias_one, "weight_two": weight_two, "bias_two": bias_two}


def conv_layer(field, kernel, bias):
    values = field.astype(jnp.float32)
    depth_n, rows_n, cols_n, chans = values.shape
    flat_count = depth_n * rows_n * cols_n
    total = jnp.zeros((flat_count, kernel.shape[3]), jnp.float32)
    for depth_tap in range(3):
        for row_tap in range(3):
            for col_tap in range(3):
                shifted = jnp.roll(values, (1 - depth_tap, 1 - row_tap, 1 - col_tap), axis=(0, 1, 2))
                total = total + jnp.dot(shifted.reshape(flat_count, chans), kernel[depth_tap, row_tap, col_tap].astype(jnp.float32).T, precision=lax.Precision.HIGHEST)
    result = jnp.maximum(total + bias[None, :], 0.0)
    return result.reshape(depth_n, rows_n, cols_n, kernel.shape[3]).astype(jnp.bfloat16)


def reference(volume, weight_one, bias_one, weight_two, bias_two):
    hidden = conv_layer(volume, weight_one, bias_one)
    output = conv_layer(hidden, weight_two, bias_two)
    depth_n, rows_n, cols_n, chans = output.shape
    return output.reshape(depth_n, rows_n * cols_n, chans).transpose(0, 2, 1)
```

```python
import jax
import jax.numpy as jnp
from jax import lax
from jax.sharding import PartitionSpec as P


def shifted_from(block, by):
    length = lax.axis_size("space")
    return lax.ppermute(block, "space", [((i + by) % length, i) for i in range(length)])


def grid_from(block, by_space, by_chan):
    spaces = lax.axis_size("space")
    chans = lax.axis_size("chan")
    pairs = []
    for s in range(spaces):
        for c in range(chans):
            source = ((s + by_space) % spaces) * chans + (c + by_chan) % chans
            pairs.append((source, s * chans + c))
    return lax.ppermute(block, ("space", "chan"), pairs)


def spatial_sum(products, rows_n, cols_n, outs):
    products = products.reshape(rows_n, cols_n, 3, 3, outs)
    summed = None
    for row_tap in range(3):
        for col_tap in range(3):
            term = jnp.roll(products[:, :, row_tap, col_tap], (1 - row_tap, 1 - col_tap), axis=(0, 1))
            summed = term if summed is None else summed + term
    return summed


def tap_products(plane, kernel_tap):
    rows_n, cols_n, count_in = plane.shape
    outs = kernel_tap.shape[2]
    return lax.dot_general(
        plane.reshape(rows_n * cols_n, count_in),
        kernel_tap.reshape(9 * outs, count_in),
        (((1,), (1,)), ((), ())),
        preferred_element_type=jnp.float32,
    )


def conv_planes(planes, kernel, bias):
    rows_n, cols_n, _ = planes[1].shape
    outs = kernel.shape[3]
    products = None
    for depth_tap in (1, 0, 2):
        term = tap_products(planes[depth_tap], kernel[depth_tap])
        products = term if products is None else products + term
    total = spatial_sum(products, rows_n, cols_n, outs)
    return jnp.maximum(total + bias, 0.0)


def per_device(volume, weight_one, bias_one, weight_two, bias_two):
    plane = volume[0]
    rows_n, cols_n, _ = plane.shape
    planes = [shifted_from(plane, -1), plane, shifted_from(plane, 1)]
    hidden = conv_planes(planes, weight_one, bias_one).astype(jnp.bfloat16)

    chans = lax.axis_size("chan")
    me = lax.axis_index("chan")
    gathered = []
    for depth_tap in range(3):
        blocks = []
        for by_chan in range(chans):
            if depth_tap == 1 and by_chan == 0:
                blocks.append(hidden)
            else:
                blocks.append(grid_from(hidden, depth_tap - 1, by_chan))
        rotated = jnp.concatenate(blocks, axis=-1)
        owned = hidden.shape[-1]
        gathered.append(jnp.roll(rotated, me * owned, axis=-1))
    output = conv_planes(gathered, weight_two, bias_two).astype(jnp.bfloat16)
    outs = output.shape[-1]
    return output.reshape(1, rows_n * cols_n, outs).transpose(0, 2, 1)


def solution(mesh):
    return jax.shard_map(
        per_device,
        mesh=mesh,
        in_specs=(
            P("space", None, None, None),
            P(None, None, None, "chan", None),
            P("chan"),
            P(None, None, None, "chan", None),
            P("chan"),
        ),
        out_specs=P("space", "chan", None),
        check_vma=False,
    )
```

```python
import jax
import jax.numpy as jnp
from jax import lax
from jax.sharding import PartitionSpec as P


def gathered_from(block, source_of):
    spaces = lax.axis_size("space")
    chans = lax.axis_size("chan")
    pairs = []
    for s in range(spaces):
        for c in range(chans):
            source_s, source_c = source_of(s, c)
            pairs.append(((source_s % spaces) * chans + source_c % chans, s * chans + c))
    return lax.ppermute(block, ("space", "chan"), pairs)


def from_side(block, distance):
    return gathered_from(block, lambda s, c: (s - distance if c % 2 == 0 else s + distance, c))


def from_chan_partner(block, bit):
    return gathered_from(block, lambda s, c: (s, c ^ bit))


def spatial_sum(products, outs):
    planes, rows_n, cols_n, _ = products.shape
    products = products.reshape(planes, rows_n, cols_n, 3, 3, outs)
    summed = None
    for row_tap in range(3):
        for col_tap in range(3):
            term = jnp.roll(products[:, :, :, row_tap, col_tap], (1 - row_tap, 1 - col_tap), axis=(1, 2))
            summed = term if summed is None else summed + term
    return summed


def conv_stack(field, kernel, bias, planes_out):
    _, rows_n, cols_n, count_in = field.shape
    outs = kernel.shape[3]
    products = None
    for depth_tap in range(3):
        window = field[depth_tap:depth_tap + planes_out].reshape(planes_out * rows_n * cols_n, count_in)
        term = lax.dot_general(
            window,
            kernel[depth_tap].reshape(9 * outs, count_in),
            (((1,), (1,)), ((), ())),
            preferred_element_type=jnp.float32,
        )
        products = term if products is None else products + term
    products = products.reshape(planes_out, rows_n, cols_n, 9 * outs)
    return jnp.maximum(spatial_sum(products, outs) + bias, 0.0)


def xor_order(held, me):
    count = len(held)
    blocks = list(held)
    bit = 1
    while bit < count:
        flip = (me & bit) != 0
        swapped = [blocks[j ^ bit] for j in range(count)]
        blocks = [jnp.where(flip, swapped[j], blocks[j]) for j in range(count)]
        bit *= 2
    return blocks


def per_device(volume, weight_one, bias_one, weight_two, bias_two):
    plane = volume[0]
    rows_n, cols_n, _ = plane.shape
    me = lax.axis_index("chan")
    chans = lax.axis_size("chan")

    near = from_side(plane, 1)
    far = from_side(plane, 2)
    mine = jnp.stack([near, far])
    theirs = from_chan_partner(mine, 1)
    odd = (me % 2) == 1
    below = jnp.where(odd, theirs, mine)
    above = jnp.where(odd, mine, theirs)
    field = jnp.stack([below[1], below[0], plane, above[0], above[1]])
    hidden = conv_stack(field, weight_one, bias_one, 3).astype(jnp.bfloat16)

    held = {0: hidden}
    bit = 1
    while bit < chans:
        bit *= 2
    bit //= 2
    while bit >= 1:
        offsets = sorted(held)
        sent = jnp.stack([held[j] for j in offsets])
        got = from_chan_partner(sent, bit)
        for position, j in enumerate(offsets):
            held[j ^ bit] = got[position]
        bit //= 2
    blocks = xor_order([held[j] for j in range(chans)], me)
    gathered = jnp.concatenate(blocks, axis=-1)
    output = conv_stack(gathered, weight_two, bias_two, 1).astype(jnp.bfloat16)
    outs = output.shape[-1]
    return output.reshape(1, rows_n * cols_n, outs).transpose(0, 2, 1)


def solution(mesh):
    return jax.shard_map(
        per_device,
        mesh=mesh,
        in_specs=(
            P("space", None, None, None),
            P(None, None, None, "chan", None),
            P("chan"),
            P(None, None, None, "chan", None),
            P("chan"),
        ),
        out_specs=P("space", "chan", None),
        check_vma=False,
    )
```

```python
import functools

import jax
import jax.numpy as jnp
from jax import lax
from jax.experimental import pallas as pl
from jax.experimental.pallas import tpu as pltpu
from jax.sharding import PartitionSpec as P


def gathered_from(block, source_of):
    spaces = lax.axis_size("space")
    chans = lax.axis_size("chan")
    pairs = []
    for s in range(spaces):
        for c in range(chans):
            source_s, source_c = source_of(s, c)
            pairs.append(((source_s % spaces) * chans + source_c % chans, s * chans + c))
    return lax.ppermute(block, ("space", "chan"), pairs)


def from_side(block, distance):
    return gathered_from(block, lambda s, c: (s - distance if c % 2 == 0 else s + distance, c))


def from_chan_partner(block, bit):
    return gathered_from(block, lambda s, c: (s, c ^ bit))


def spatial_epilogue(acc_ref, plane, rows_n, cols_n, outs, bias):
    cells = rows_n * cols_n
    base = plane * cells
    column = lax.broadcasted_iota(jnp.int32, (cells, outs), 0) % cols_n
    total = None
    for col_tap in range(3):
        shifted = None
        for row_tap in range(3):
            tap = row_tap * 3 + col_tap
            part = acc_ref[pl.ds(base, cells), pl.ds(tap * outs, outs)]
            amount = ((1 - row_tap) * cols_n) % cells
            if amount:
                part = pltpu.roll(part, amount, 0)
            shifted = part if shifted is None else shifted + part
        if col_tap == 0:
            shifted = jnp.where(
                column == 0,
                pltpu.roll(shifted, (1 - cols_n) % cells, 0),
                pltpu.roll(shifted, 1, 0),
            )
        elif col_tap == 2:
            shifted = jnp.where(
                column == cols_n - 1,
                pltpu.roll(shifted, cols_n - 1, 0),
                pltpu.roll(shifted, cells - 1, 0),
            )
        total = shifted if total is None else total + shifted
    return jnp.maximum(total + bias, 0.0)


def conv_kernel(fill, planes_out, rows_n, cols_n, transpose_out, *refs):
    flag_ref = refs[0]
    w_ref, b_ref, o_ref, field_ref, acc_ref = refs[-5:]
    inputs = refs[1:-5]
    depth_tap = pl.program_id(0)
    cells = rows_n * cols_n
    outs = b_ref.shape[1]

    @pl.when(depth_tap == 0)
    def _():
        fill(flag_ref[0], inputs, field_ref)

    window = field_ref[pl.ds(depth_tap, planes_out)]
    window = window.reshape(planes_out * cells, window.shape[-1])
    products = lax.dot_general(
        window, w_ref[0], (((1,), (1,)), ((), ())), preferred_element_type=jnp.float32
    )

    @pl.when(depth_tap == 0)
    def _():
        acc_ref[...] = products

    @pl.when(depth_tap > 0)
    def _():
        acc_ref[...] += products

    @pl.when(depth_tap == 2)
    def _():
        bias = b_ref[...]
        for plane in range(planes_out):
            result = spatial_epilogue(acc_ref, plane, rows_n, cols_n, outs, bias)
            if transpose_out:
                o_ref[plane] = result.T.astype(o_ref.dtype)
            else:
                o_ref[plane] = result.astype(o_ref.dtype)


def conv_call(fill, flag, inputs, kernel, bias, field_shape, planes_out, rows_n, cols_n, transpose_out):
    outs = kernel.shape[3]
    count_in = kernel.shape[4]
    cells = rows_n * cols_n
    stacked = kernel.reshape(3, 9 * outs, count_in)
    in_specs = [pl.BlockSpec(x.shape, lambda a, f, n=x.ndim: (0,) * n) for x in inputs]
    in_specs.append(pl.BlockSpec((1, 9 * outs, count_in), lambda a, f: (a, 0, 0)))
    in_specs.append(pl.BlockSpec((1, outs), lambda a, f: (0, 0)))
    out_shape = (planes_out, outs, cells) if transpose_out else (planes_out, cells, outs)
    flops = 2 * 3 * planes_out * cells * count_in * 9 * outs
    moved = stacked.size * 2 + sum(x.size * 2 for x in inputs) + planes_out * cells * outs * 2
    return pl.pallas_call(
        functools.partial(conv_kernel, fill, planes_out, rows_n, cols_n, transpose_out),
        out_shape=jax.ShapeDtypeStruct(out_shape, jnp.bfloat16),
        grid_spec=pltpu.PrefetchScalarGridSpec(
            num_scalar_prefetch=1,
            grid=(3,),
            in_specs=in_specs,
            out_specs=pl.BlockSpec(out_shape, lambda a, f: (0, 0, 0)),
            scratch_shapes=[
                pltpu.VMEM(field_shape, jnp.bfloat16),
                pltpu.VMEM((planes_out * cells, 9 * outs), jnp.float32),
            ],
        ),
        compiler_params=pltpu.CompilerParams(
            dimension_semantics=("arbitrary",), vmem_limit_bytes=48 * 1024 * 1024
        ),
        cost_estimate=pl.CostEstimate(flops=flops, transcendentals=0, bytes_accessed=moved),
    )(flag, *inputs, stacked, bias.reshape(1, outs))


def fill_volume(odd, inputs, field_ref):
    own, mine, theirs = inputs
    is_odd = odd != 0
    below = jnp.where(is_odd, theirs[...], mine[...])
    above = jnp.where(is_odd, mine[...], theirs[...])
    field_ref[0] = below[1]
    field_ref[1] = below[0]
    field_ref[2] = own[...]
    field_ref[3] = above[0]
    field_ref[4] = above[1]


def fill_hidden(layout, me, inputs, field_ref):
    blocks = {}
    for ref, offsets in zip(inputs, layout):
        for position, j in enumerate(offsets):
            blocks[j] = ref[position]
    count = len(blocks)
    ordered = [blocks[j] for j in range(count)]
    bit = 1
    while bit < count:
        flip = (me & bit) != 0
        ordered = [jnp.where(flip, ordered[j ^ bit], ordered[j]) for j in range(count)]
        bit *= 2
    owned = ordered[0].shape[-1]
    for position in range(count):
        field_ref[:, :, pl.ds(position * owned, owned)] = ordered[position]


def per_device(volume, weight_one, bias_one, weight_two, bias_two):
    plane = volume[0]
    rows_n, cols_n, count_in = plane.shape
    cells = rows_n * cols_n
    me = lax.axis_index("chan")
    chans = lax.axis_size("chan")

    flat = plane.reshape(cells, count_in)
    mine = jnp.stack([from_side(flat, 1), from_side(flat, 2)])
    theirs = from_chan_partner(mine, 1)
    odd = (me % 2).astype(jnp.int32).reshape(1)
    hidden = conv_call(
        fill_volume, odd, [flat, mine, theirs], weight_one, bias_one,
        (5, cells, count_in), 3, rows_n, cols_n, False,
    )

    held = [(hidden[None], (0,))]
    offsets = [0]
    bit = 1
    while bit < chans:
        bit *= 2
    bit //= 2
    while bit >= 1:
        sent = jnp.stack([blk for arr, offs in held for blk in [arr[i] for i in range(len(offs))]])
        got = from_chan_partner(sent, bit)
        held.append((got, tuple(j ^ bit for j in offsets)))
        offsets = offsets + [j ^ bit for j in offsets]
        bit //= 2
    layout = tuple(offs for _, offs in held)
    inputs = [arr for arr, _ in held]
    me_flag = me.astype(jnp.int32).reshape(1)
    output = conv_call(
        functools.partial(fill_hidden, layout), me_flag, inputs, weight_two, bias_two,
        (3, cells, count_in), 1, rows_n, cols_n, True,
    )
    return output


def solution(mesh):
    return jax.shard_map(
        per_device,
        mesh=mesh,
        in_specs=(
            P("space", None, None, None),
            P(None, None, None, "chan", None),
            P("chan"),
            P(None, None, None, "chan", None),
            P("chan"),
        ),
        out_specs=P("space", "chan", None),
        check_vma=False,
    )
```

```python
import functools

import jax
import jax.numpy as jnp
from jax import lax
from jax.experimental import pallas as pl
from jax.experimental.pallas import tpu as pltpu
from jax.sharding import PartitionSpec as P


def gathered_from(block, source_of):
    spaces = lax.axis_size("space")
    chans = lax.axis_size("chan")
    pairs = []
    for s in range(spaces):
        for c in range(chans):
            source_s, source_c = source_of(s, c)
            pairs.append(((source_s % spaces) * chans + source_c % chans, s * chans + c))
    return lax.ppermute(block, ("space", "chan"), pairs)


def from_side(block, distance):
    return gathered_from(block, lambda s, c: (s - distance if c % 2 == 0 else s + distance, c))


def from_chan_partner(block, bit):
    return gathered_from(block, lambda s, c: (s, c ^ bit))


def spatial_sum(acc_ref, plane, rows_n, cols_n, outs):
    cells = rows_n * cols_n
    column = lax.broadcasted_iota(jnp.int32, (cells, outs), 0) % cols_n
    total = None
    for col_tap in range(3):
        shifted = None
        for row_tap in range(3):
            tap = row_tap * 3 + col_tap
            part = acc_ref[plane, :, pl.ds(tap * outs, outs)]
            amount = ((1 - row_tap) * cols_n) % cells
            if amount:
                part = pltpu.roll(part, amount, 0)
            shifted = part if shifted is None else shifted + part
        if col_tap == 0:
            shifted = jnp.where(
                column == 0,
                pltpu.roll(shifted, (1 - cols_n) % cells, 0),
                pltpu.roll(shifted, 1, 0),
            )
        elif col_tap == 2:
            shifted = jnp.where(
                column == cols_n - 1,
                pltpu.roll(shifted, cols_n - 1, 0),
                pltpu.roll(shifted, cells - 1, 0),
            )
        total = shifted if total is None else total + shifted
    return total


def tap_product(plane, w_ref, depth_tap):
    return lax.dot_general(
        plane, w_ref[depth_tap], (((1,), (1,)), ((), ())), preferred_element_type=jnp.float32
    )


def own_plane_kernel(rows_n, cols_n, x_ref, w_ref, o_ref, acc_ref):
    outs = o_ref.shape[2]
    x = x_ref[...]
    for plane in range(3):
        acc_ref[plane] = tap_product(x, w_ref, 2 - plane)
    for plane in range(3):
        o_ref[plane] = spatial_sum(acc_ref, plane, rows_n, cols_n, outs)


def neighbour_kernel(rows_n, cols_n, odd_ref, mine_ref, theirs_ref, part_ref, w_ref, b_ref, o_ref, acc_ref):
    outs = o_ref.shape[2]
    is_odd = odd_ref[0] != 0

    def side(below, index):
        if below:
            return jnp.where(is_odd, theirs_ref[index], mine_ref[index])
        return jnp.where(is_odd, mine_ref[index], theirs_ref[index])

    minus_one, minus_two = side(True, 0), side(True, 1)
    plus_one, plus_two = side(False, 0), side(False, 1)
    acc_ref[0] = tap_product(minus_two, w_ref, 0) + tap_product(minus_one, w_ref, 1)
    acc_ref[1] = tap_product(minus_one, w_ref, 0) + tap_product(plus_one, w_ref, 2)
    acc_ref[2] = tap_product(plus_one, w_ref, 1) + tap_product(plus_two, w_ref, 2)
    bias = b_ref[...]
    for plane in range(3):
        total = spatial_sum(acc_ref, plane, rows_n, cols_n, outs) + part_ref[plane]
        o_ref[plane] = jnp.maximum(total + bias, 0.0).astype(o_ref.dtype)


def second_kernel(rows_n, cols_n, layout, me_ref, *refs):
    inputs = refs[:len(layout)]
    w_ref, b_ref, o_ref, field_ref, acc_ref = refs[len(layout):]
    outs = b_ref.shape[1]
    me = me_ref[0]
    blocks = {}
    for ref, offsets in zip(inputs, layout):
        for position, j in enumerate(offsets):
            blocks[j] = ref[position]
    count = len(blocks)
    ordered = [blocks[j] for j in range(count)]
    bit = 1
    while bit < count:
        flip = (me & bit) != 0
        ordered = [jnp.where(flip, ordered[j ^ bit], ordered[j]) for j in range(count)]
        bit *= 2
    for position in range(count):
        field_ref[:, :, pl.ds(position * outs, outs)] = ordered[position]
    products = None
    for depth_tap in range(3):
        term = tap_product(field_ref[depth_tap], w_ref, depth_tap)
        products = term if products is None else products + term
    acc_ref[0] = products
    total = spatial_sum(acc_ref, 0, rows_n, cols_n, outs)
    result = jnp.maximum(total + b_ref[...], 0.0)
    o_ref[0] = result.T.astype(o_ref.dtype)


def vmem_call(kernel, out_shape, operands, scratch, flops, smem_first=False):
    specs = [pl.BlockSpec(memory_space=pltpu.VMEM) for _ in operands]
    if smem_first:
        specs[0] = pl.BlockSpec(memory_space=pltpu.SMEM)
    moved = sum(x.size * x.dtype.itemsize for x in operands) + out_shape.size * out_shape.dtype.itemsize
    return pl.pallas_call(
        kernel,
        out_shape=out_shape,
        in_specs=specs,
        out_specs=pl.BlockSpec(memory_space=pltpu.VMEM),
        scratch_shapes=scratch,
        compiler_params=pltpu.CompilerParams(vmem_limit_bytes=48 * 1024 * 1024),
        cost_estimate=pl.CostEstimate(flops=flops, transcendentals=0, bytes_accessed=moved),
    )(*operands)


def per_device(volume, weight_one, bias_one, weight_two, bias_two):
    plane = volume[0]
    rows_n, cols_n, count_in = plane.shape
    cells = rows_n * cols_n
    outs = weight_one.shape[3]
    me = lax.axis_index("chan")
    chans = lax.axis_size("chan")
    one_stack = weight_one.reshape(3, 9 * outs, count_in)
    two_stack = weight_two.reshape(3, 9 * outs, count_in)
    tap_flops = 2 * cells * count_in * 9 * outs

    flat = plane.reshape(cells, count_in)
    near, far = from_side(flat, 1), from_side(flat, 2)
    own_terms = vmem_call(
        functools.partial(own_plane_kernel, rows_n, cols_n),
        jax.ShapeDtypeStruct((3, cells, outs), jnp.float32),
        [flat, one_stack],
        [pltpu.VMEM((3, cells, 9 * outs), jnp.float32)],
        3 * tap_flops,
    )
    near, far, own_terms = lax.optimization_barrier((near, far, own_terms))
    mine = jnp.stack([near, far])
    theirs = from_chan_partner(mine, 1)
    odd = (me % 2).astype(jnp.int32).reshape(1)
    hidden = vmem_call(
        functools.partial(neighbour_kernel, rows_n, cols_n),
        jax.ShapeDtypeStruct((3, cells, outs), jnp.bfloat16),
        [odd, mine, theirs, own_terms, one_stack, bias_one.reshape(1, outs)],
        [pltpu.VMEM((3, cells, 9 * outs), jnp.float32)],
        6 * tap_flops,
        smem_first=True,
    )

    held = [(hidden[None], (0,))]
    offsets = [0]
    bit = 1
    while bit < chans:
        bit *= 2
    bit //= 2
    while bit >= 1:
        sent = jnp.stack([arr[i] for arr, offs in held for i in range(len(offs))])
        got = from_chan_partner(sent, bit)
        held.append((got, tuple(j ^ bit for j in offsets)))
        offsets = offsets + [j ^ bit for j in offsets]
        bit //= 2
    layout = tuple(offs for _, offs in held)
    me_flag = me.astype(jnp.int32).reshape(1)
    output = vmem_call(
        functools.partial(second_kernel, rows_n, cols_n, layout),
        jax.ShapeDtypeStruct((1, outs, cells), jnp.bfloat16),
        [me_flag] + [arr for arr, _ in held] + [two_stack, bias_two.reshape(1, outs)],
        [pltpu.VMEM((3, cells, count_in), jnp.bfloat16), pltpu.VMEM((1, cells, 9 * outs), jnp.float32)],
        3 * tap_flops,
        smem_first=True,
    )
    return output


def solution(mesh):
    return jax.shard_map(
        per_device,
        mesh=mesh,
        in_specs=(
            P("space", None, None, None),
            P(None, None, None, "chan", None),
            P("chan"),
            P(None, None, None, "chan", None),
            P("chan"),
        ),
        out_specs=P("space", "chan", None),
        check_vma=False,
    )
```

```python
import functools

import jax
import jax.numpy as jnp
from jax import lax
from jax.experimental import pallas as pl
from jax.experimental.pallas import tpu as pltpu
from jax.sharding import PartitionSpec as P


def gathered_from(block, source_of):
    spaces = lax.axis_size("space")
    chans = lax.axis_size("chan")
    pairs = []
    for s in range(spaces):
        for c in range(chans):
            source_s, source_c = source_of(s, c)
            pairs.append(((source_s % spaces) * chans + source_c % chans, s * chans + c))
    return lax.ppermute(block, ("space", "chan"), pairs)


def from_side(block, distance):
    return gathered_from(block, lambda s, c: (s - distance if c % 2 == 0 else s + distance, c))


def from_chan_partner(block, bit):
    return gathered_from(block, lambda s, c: (s, c ^ bit))


def spatial_sum(acc_ref, plane, rows_n, cols_n, outs):
    cells = rows_n * cols_n
    column = lax.broadcasted_iota(jnp.int32, (cells, outs), 0) % cols_n
    total = None
    for col_tap in range(3):
        shifted = None
        for row_tap in range(3):
            tap = row_tap * 3 + col_tap
            part = acc_ref[plane, :, pl.ds(tap * outs, outs)]
            amount = ((1 - row_tap) * cols_n) % cells
            if amount:
                part = pltpu.roll(part, amount, 0)
            shifted = part if shifted is None else shifted + part
        if col_tap == 0:
            shifted = jnp.where(
                column == 0,
                pltpu.roll(shifted, (1 - cols_n) % cells, 0),
                pltpu.roll(shifted, 1, 0),
            )
        elif col_tap == 2:
            shifted = jnp.where(
                column == cols_n - 1,
                pltpu.roll(shifted, cols_n - 1, 0),
                pltpu.roll(shifted, cells - 1, 0),
            )
        total = shifted if total is None else total + shifted
    return total


def tap_product(plane, w_ref, depth_tap):
    return lax.dot_general(
        plane, w_ref[depth_tap], (((1,), (1,)), ((), ())), preferred_element_type=jnp.float32
    )


def own_plane_kernel(rows_n, cols_n, x_ref, w_ref, o_ref, acc_ref):
    outs = o_ref.shape[2]
    x = x_ref[...]
    for plane in range(3):
        acc_ref[plane] = tap_product(x, w_ref, 2 - plane)
    for plane in range(3):
        o_ref[plane] = spatial_sum(acc_ref, plane, rows_n, cols_n, outs)


def neighbour_kernel(rows_n, cols_n, odd_ref, near_ref, far_ref, their_near_ref, their_far_ref, part_ref,
                     w_ref, b_ref, o_ref, acc_ref):
    outs = o_ref.shape[2]
    is_odd = odd_ref[0] != 0
    minus_one = jnp.where(is_odd, their_near_ref[...], near_ref[...])
    minus_two = jnp.where(is_odd, their_far_ref[...], far_ref[...])
    plus_one = jnp.where(is_odd, near_ref[...], their_near_ref[...])
    plus_two = jnp.where(is_odd, far_ref[...], their_far_ref[...])
    acc_ref[0] = tap_product(minus_two, w_ref, 0) + tap_product(minus_one, w_ref, 1)
    acc_ref[1] = tap_product(minus_one, w_ref, 0) + tap_product(plus_one, w_ref, 2)
    acc_ref[2] = tap_product(plus_one, w_ref, 1) + tap_product(plus_two, w_ref, 2)
    bias = b_ref[...]
    for plane in range(3):
        total = spatial_sum(acc_ref, plane, rows_n, cols_n, outs) + part_ref[plane]
        o_ref[plane] = jnp.maximum(total + bias, 0.0).astype(o_ref.dtype)


def second_kernel(rows_n, cols_n, layout, me_ref, *refs):
    inputs = refs[:len(layout)]
    w_ref, b_ref, o_ref, field_ref, acc_ref = refs[len(layout):]
    outs = b_ref.shape[1]
    me = me_ref[0]
    blocks = {}
    for ref, offsets in zip(inputs, layout):
        for position, j in enumerate(offsets):
            blocks[j] = ref[position]
    count = len(blocks)
    ordered = [blocks[j] for j in range(count)]
    bit = 1
    while bit < count:
        flip = (me & bit) != 0
        ordered = [jnp.where(flip, ordered[j ^ bit], ordered[j]) for j in range(count)]
        bit *= 2
    for position in range(count):
        field_ref[:, :, pl.ds(position * outs, outs)] = ordered[position]
    products = None
    for depth_tap in range(3):
        term = tap_product(field_ref[depth_tap], w_ref, depth_tap)
        products = term if products is None else products + term
    acc_ref[0] = products
    total = spatial_sum(acc_ref, 0, rows_n, cols_n, outs)
    result = jnp.maximum(total + b_ref[...], 0.0)
    o_ref[0] = result.T.astype(o_ref.dtype)


def vmem_call(kernel, out_shape, operands, scratch, flops, smem_first=False):
    specs = [pl.BlockSpec(memory_space=pltpu.VMEM) for _ in operands]
    if smem_first:
        specs[0] = pl.BlockSpec(memory_space=pltpu.SMEM)
    moved = sum(x.size * x.dtype.itemsize for x in operands) + out_shape.size * out_shape.dtype.itemsize
    return pl.pallas_call(
        kernel,
        out_shape=out_shape,
        in_specs=specs,
        out_specs=pl.BlockSpec(memory_space=pltpu.VMEM),
        scratch_shapes=scratch,
        compiler_params=pltpu.CompilerParams(vmem_limit_bytes=48 * 1024 * 1024),
        cost_estimate=pl.CostEstimate(flops=flops, transcendentals=0, bytes_accessed=moved),
    )(*operands)


def per_device(volume, weight_one, bias_one, weight_two, bias_two):
    plane = volume[0]
    rows_n, cols_n, count_in = plane.shape
    cells = rows_n * cols_n
    outs = weight_one.shape[3]
    me = lax.axis_index("chan")
    chans = lax.axis_size("chan")
    one_stack = weight_one.reshape(3, 9 * outs, count_in)
    two_stack = weight_two.reshape(3, 9 * outs, count_in)
    tap_flops = 2 * cells * count_in * 9 * outs

    flat = plane.reshape(cells, count_in)
    near, far = from_side(flat, 1), from_side(flat, 2)
    own_terms = vmem_call(
        functools.partial(own_plane_kernel, rows_n, cols_n),
        jax.ShapeDtypeStruct((3, cells, outs), jnp.float32),
        [flat, one_stack],
        [pltpu.VMEM((3, cells, 9 * outs), jnp.float32)],
        3 * tap_flops,
    )
    near, far, own_terms = lax.optimization_barrier((near, far, own_terms))
    their_near, their_far = from_chan_partner(near, 1), from_chan_partner(far, 1)
    odd = (me % 2).astype(jnp.int32).reshape(1)
    hidden = vmem_call(
        functools.partial(neighbour_kernel, rows_n, cols_n),
        jax.ShapeDtypeStruct((3, cells, outs), jnp.bfloat16),
        [odd, near, far, their_near, their_far, own_terms, one_stack, bias_one.reshape(1, outs)],
        [pltpu.VMEM((3, cells, 9 * outs), jnp.float32)],
        6 * tap_flops,
        smem_first=True,
    )

    held = [(hidden[None], (0,))]
    offsets = [0]
    bit = 1
    while bit < chans:
        bit *= 2
    bit //= 2
    while bit >= 1:
        sent = jnp.stack([arr[i] for arr, offs in held for i in range(len(offs))])
        got = from_chan_partner(sent, bit)
        held.append((got, tuple(j ^ bit for j in offsets)))
        offsets = offsets + [j ^ bit for j in offsets]
        bit //= 2
    layout = tuple(offs for _, offs in held)
    me_flag = me.astype(jnp.int32).reshape(1)
    output = vmem_call(
        functools.partial(second_kernel, rows_n, cols_n, layout),
        jax.ShapeDtypeStruct((1, outs, cells), jnp.bfloat16),
        [me_flag] + [arr for arr, _ in held] + [two_stack, bias_two.reshape(1, outs)],
        [pltpu.VMEM((3, cells, count_in), jnp.bfloat16), pltpu.VMEM((1, cells, 9 * outs), jnp.float32)],
        3 * tap_flops,
        smem_first=True,
    )
    return output


def solution(mesh):
    return jax.shard_map(
        per_device,
        mesh=mesh,
        in_specs=(
            P("space", None, None, None),
            P(None, None, None, "chan", None),
            P("chan"),
            P(None, None, None, "chan", None),
            P("chan"),
        ),
        out_specs=P("space", "chan", None),
        check_vma=False,
    )
```

```python
import functools

import jax
import jax.numpy as jnp
from jax import lax
from jax.experimental import pallas as pl
from jax.experimental.pallas import tpu as pltpu
from jax.sharding import PartitionSpec as P


def gathered_from(block, source_of):
    spaces = lax.axis_size("space")
    chans = lax.axis_size("chan")
    pairs = []
    for s in range(spaces):
        for c in range(chans):
            source_s, source_c = source_of(s, c)
            pairs.append(((source_s % spaces) * chans + source_c % chans, s * chans + c))
    return lax.ppermute(block, ("space", "chan"), pairs)


def from_side(block, distance):
    return gathered_from(block, lambda s, c: (s - distance if c % 2 == 0 else s + distance, c))


def from_chan_partner(block, bit):
    return gathered_from(block, lambda s, c: (s, c ^ bit))


def spatial_sum(acc_ref, plane, rows_n, cols_n, outs):
    cells = rows_n * cols_n
    column = lax.broadcasted_iota(jnp.int32, (cells, outs), 0) % cols_n
    total = None
    for col_tap in range(3):
        shifted = None
        for row_tap in range(3):
            tap = row_tap * 3 + col_tap
            part = acc_ref[plane, :, pl.ds(tap * outs, outs)]
            amount = ((1 - row_tap) * cols_n) % cells
            if amount:
                part = pltpu.roll(part, amount, 0)
            shifted = part if shifted is None else shifted + part
        if col_tap == 0:
            shifted = jnp.where(
                column == 0,
                pltpu.roll(shifted, (1 - cols_n) % cells, 0),
                pltpu.roll(shifted, 1, 0),
            )
        elif col_tap == 2:
            shifted = jnp.where(
                column == cols_n - 1,
                pltpu.roll(shifted, cols_n - 1, 0),
                pltpu.roll(shifted, cells - 1, 0),
            )
        total = shifted if total is None else total + shifted
    return total


def tap_product(plane, w_ref, depth_tap):
    return lax.dot_general(
        plane, w_ref[depth_tap], (((1,), (1,)), ((), ())), preferred_element_type=jnp.float32
    )


def own_plane_kernel(rows_n, cols_n, x_ref, w_ref, o_ref, acc_ref):
    outs = o_ref.shape[2]
    x = x_ref[...]
    for plane in range(3):
        acc_ref[plane] = tap_product(x, w_ref, 2 - plane)
    for plane in range(3):
        o_ref[plane] = spatial_sum(acc_ref, plane, rows_n, cols_n, outs)


def neighbour_kernel(rows_n, cols_n, odd_ref, near_ref, far_ref, their_near_ref, their_far_ref, part_ref,
                     w_ref, b_ref, o_ref, acc_ref):
    outs = o_ref.shape[2]

    def accumulate(minus_one, minus_two, plus_one, plus_two):
        acc_ref[0] = tap_product(minus_two[...], w_ref, 0) + tap_product(minus_one[...], w_ref, 1)
        acc_ref[1] = tap_product(minus_one[...], w_ref, 0) + tap_product(plus_one[...], w_ref, 2)
        acc_ref[2] = tap_product(plus_one[...], w_ref, 1) + tap_product(plus_two[...], w_ref, 2)

    @pl.when(odd_ref[0] == 0)
    def _():
        accumulate(near_ref, far_ref, their_near_ref, their_far_ref)

    @pl.when(odd_ref[0] != 0)
    def _():
        accumulate(their_near_ref, their_far_ref, near_ref, far_ref)

    bias = b_ref[...]
    for plane in range(3):
        total = spatial_sum(acc_ref, plane, rows_n, cols_n, outs) + part_ref[plane]
        o_ref[plane] = jnp.maximum(total + bias, 0.0).astype(o_ref.dtype)


def second_kernel(rows_n, cols_n, layout, me_ref, *refs):
    inputs = refs[:len(layout)]
    w_ref, b_ref, o_ref, field_ref, acc_ref = refs[len(layout):]
    outs = b_ref.shape[1]
    me = me_ref[0]
    blocks = {}
    for ref, offsets in zip(inputs, layout):
        for position, j in enumerate(offsets):
            blocks[j] = (ref, position)
    count = len(blocks)
    for index in range(count):

        @pl.when(me == index)
        def _():
            for j in range(count):
                ref, position = blocks[j]
                field_ref[:, :, pl.ds((index ^ j) * outs, outs)] = ref[position]
    products = None
    for depth_tap in range(3):
        term = tap_product(field_ref[depth_tap], w_ref, depth_tap)
        products = term if products is None else products + term
    acc_ref[0] = products
    total = spatial_sum(acc_ref, 0, rows_n, cols_n, outs)
    result = jnp.maximum(total + b_ref[...], 0.0)
    o_ref[0] = result.T.astype(o_ref.dtype)


def vmem_call(kernel, out_shape, operands, scratch, flops, smem_first=False):
    specs = [pl.BlockSpec(memory_space=pltpu.VMEM) for _ in operands]
    if smem_first:
        specs[0] = pl.BlockSpec(memory_space=pltpu.SMEM)
    moved = sum(x.size * x.dtype.itemsize for x in operands) + out_shape.size * out_shape.dtype.itemsize
    return pl.pallas_call(
        kernel,
        out_shape=out_shape,
        in_specs=specs,
        out_specs=pl.BlockSpec(memory_space=pltpu.VMEM),
        scratch_shapes=scratch,
        compiler_params=pltpu.CompilerParams(vmem_limit_bytes=48 * 1024 * 1024),
        cost_estimate=pl.CostEstimate(flops=flops, transcendentals=0, bytes_accessed=moved),
    )(*operands)


def per_device(volume, weight_one, bias_one, weight_two, bias_two):
    plane = volume[0]
    rows_n, cols_n, count_in = plane.shape
    cells = rows_n * cols_n
    outs = weight_one.shape[3]
    me = lax.axis_index("chan")
    chans = lax.axis_size("chan")
    one_stack = weight_one.reshape(3, 9 * outs, count_in)
    two_stack = weight_two.reshape(3, 9 * outs, count_in)
    tap_flops = 2 * cells * count_in * 9 * outs

    flat = plane.reshape(cells, count_in)
    near, far = from_side(flat, 1), from_side(flat, 2)
    own_terms = vmem_call(
        functools.partial(own_plane_kernel, rows_n, cols_n),
        jax.ShapeDtypeStruct((3, cells, outs), jnp.float32),
        [flat, one_stack],
        [pltpu.VMEM((3, cells, 9 * outs), jnp.float32)],
        3 * tap_flops,
    )
    near, far, own_terms = lax.optimization_barrier((near, far, own_terms))
    their_near, their_far = from_chan_partner(near, 1), from_chan_partner(far, 1)
    odd = (me % 2).astype(jnp.int32).reshape(1)
    hidden = vmem_call(
        functools.partial(neighbour_kernel, rows_n, cols_n),
        jax.ShapeDtypeStruct((3, cells, outs), jnp.bfloat16),
        [odd, near, far, their_near, their_far, own_terms, one_stack, bias_one.reshape(1, outs)],
        [pltpu.VMEM((3, cells, 9 * outs), jnp.float32)],
        6 * tap_flops,
        smem_first=True,
    )

    held = [(hidden[None], (0,))]
    offsets = [0]
    bit = 1
    while bit < chans:
        bit *= 2
    bit //= 2
    while bit >= 1:
        sent = jnp.stack([arr[i] for arr, offs in held for i in range(len(offs))])
        got = from_chan_partner(sent, bit)
        held.append((got, tuple(j ^ bit for j in offsets)))
        offsets = offsets + [j ^ bit for j in offsets]
        bit //= 2
    layout = tuple(offs for _, offs in held)
    me_flag = me.astype(jnp.int32).reshape(1)
    output = vmem_call(
        functools.partial(second_kernel, rows_n, cols_n, layout),
        jax.ShapeDtypeStruct((1, outs, cells), jnp.bfloat16),
        [me_flag] + [arr for arr, _ in held] + [two_stack, bias_two.reshape(1, outs)],
        [pltpu.VMEM((3, cells, count_in), jnp.bfloat16), pltpu.VMEM((1, cells, 9 * outs), jnp.float32)],
        3 * tap_flops,
        smem_first=True,
    )
    return output


def solution(mesh):
    return jax.shard_map(
        per_device,
        mesh=mesh,
        in_specs=(
            P("space", None, None, None),
            P(None, None, None, "chan", None),
            P("chan"),
            P(None, None, None, "chan", None),
            P("chan"),
        ),
        out_specs=P("space", "chan", None),
        check_vma=False,
    )
```

```python
import functools

import jax
import jax.numpy as jnp
from jax import lax
from jax.experimental import pallas as pl
from jax.experimental.pallas import tpu as pltpu
from jax.sharding import PartitionSpec as P


def gathered_from(block, source_of):
    spaces = lax.axis_size("space")
    chans = lax.axis_size("chan")
    pairs = []
    for s in range(spaces):
        for c in range(chans):
            source_s, source_c = source_of(s, c)
            pairs.append(((source_s % spaces) * chans + source_c % chans, s * chans + c))
    return lax.ppermute(block, ("space", "chan"), pairs)


def from_side(block, distance):
    return gathered_from(block, lambda s, c: (s - distance if c % 2 == 0 else s + distance, c))


def from_chan_partner(block, bit):
    return gathered_from(block, lambda s, c: (s, c ^ bit))


def spatial_sum(acc_ref, plane, rows_n, cols_n, outs):
    cells = rows_n * cols_n
    column = lax.broadcasted_iota(jnp.int32, (cells, outs), 0) % cols_n
    total = None
    for col_tap in range(3):
        shifted = None
        for row_tap in range(3):
            tap = row_tap * 3 + col_tap
            part = acc_ref[plane, :, pl.ds(tap * outs, outs)]
            amount = ((1 - row_tap) * cols_n) % cells
            if amount:
                part = pltpu.roll(part, amount, 0)
            shifted = part if shifted is None else shifted + part
        if col_tap == 0:
            shifted = jnp.where(
                column == 0,
                pltpu.roll(shifted, (1 - cols_n) % cells, 0),
                pltpu.roll(shifted, 1, 0),
            )
        elif col_tap == 2:
            shifted = jnp.where(
                column == cols_n - 1,
                pltpu.roll(shifted, cols_n - 1, 0),
                pltpu.roll(shifted, cells - 1, 0),
            )
        total = shifted if total is None else total + shifted
    return total


def tap_product(plane, w_ref, depth_tap):
    return lax.dot_general(
        plane, w_ref[depth_tap], (((1,), (1,)), ((), ())), preferred_element_type=jnp.float32
    )


def own_plane_kernel(rows_n, cols_n, x_ref, w_ref, o_ref, acc_ref):
    outs = o_ref.shape[2]
    x = x_ref[...]
    for plane in range(3):
        acc_ref[plane] = tap_product(x, w_ref, 2 - plane)
    for plane in range(3):
        o_ref[plane] = spatial_sum(acc_ref, plane, rows_n, cols_n, outs)


def neighbour_kernel(rows_n, cols_n, odd_ref, near_ref, far_ref, their_near_ref, their_far_ref, part_ref,
                     w_ref, b_ref, o_ref, acc_ref):
    outs = o_ref.shape[2]
    is_odd = odd_ref[0] != 0
    minus_one = jnp.where(is_odd, their_near_ref[...], near_ref[...])
    minus_two = jnp.where(is_odd, their_far_ref[...], far_ref[...])
    plus_one = jnp.where(is_odd, near_ref[...], their_near_ref[...])
    plus_two = jnp.where(is_odd, far_ref[...], their_far_ref[...])
    acc_ref[0] = tap_product(minus_two, w_ref, 0) + tap_product(minus_one, w_ref, 1)
    acc_ref[1] = tap_product(minus_one, w_ref, 0) + tap_product(plus_one, w_ref, 2)
    acc_ref[2] = tap_product(plus_one, w_ref, 1) + tap_product(plus_two, w_ref, 2)
    bias = b_ref[...]
    for plane in range(3):
        total = spatial_sum(acc_ref, plane, rows_n, cols_n, outs) + part_ref[plane]
        o_ref[plane] = jnp.maximum(total + bias, 0.0).astype(o_ref.dtype)


def second_kernel(rows_n, cols_n, layout, me_ref, *refs):
    inputs = refs[:len(layout)]
    w_ref, b_ref, o_ref, field_ref, acc_ref = refs[len(layout):]
    outs = b_ref.shape[1]
    me = me_ref[0]
    blocks = {}
    for ref, offsets in zip(inputs, layout):
        for position, j in enumerate(offsets):
            blocks[j] = ref[position]
    count = len(blocks)
    ordered = [blocks[j] for j in range(count)]
    bit = 1
    while bit < count:
        flip = (me & bit) != 0
        ordered = [jnp.where(flip, ordered[j ^ bit], ordered[j]) for j in range(count)]
        bit *= 2
    for position in range(count):
        field_ref[:, :, pl.ds(position * outs, outs)] = ordered[position]
    products = None
    for depth_tap in range(3):
        term = tap_product(field_ref[depth_tap], w_ref, depth_tap)
        products = term if products is None else products + term
    acc_ref[0] = products
    total = spatial_sum(acc_ref, 0, rows_n, cols_n, outs)
    result = jnp.maximum(total + b_ref[...], 0.0)
    o_ref[0] = result.T.astype(o_ref.dtype)


def vmem_call(kernel, out_shape, operands, scratch, flops, smem_first=False):
    specs = [pl.BlockSpec(memory_space=pltpu.VMEM) for _ in operands]
    if smem_first:
        specs[0] = pl.BlockSpec(memory_space=pltpu.SMEM)
    moved = sum(x.size * x.dtype.itemsize for x in operands) + out_shape.size * out_shape.dtype.itemsize
    return pl.pallas_call(
        kernel,
        out_shape=out_shape,
        in_specs=specs,
        out_specs=pl.BlockSpec(memory_space=pltpu.VMEM),
        scratch_shapes=scratch,
        compiler_params=pltpu.CompilerParams(vmem_limit_bytes=48 * 1024 * 1024),
        cost_estimate=pl.CostEstimate(flops=flops, transcendentals=0, bytes_accessed=moved),
    )(*operands)


def per_device(volume, weight_one, bias_one, weight_two, bias_two):
    plane = volume[0]
    rows_n, cols_n, count_in = plane.shape
    cells = rows_n * cols_n
    outs = weight_one.shape[3]
    me = lax.axis_index("chan")
    chans = lax.axis_size("chan")
    one_stack = weight_one.reshape(3, 9 * outs, count_in)
    two_stack = weight_two.reshape(3, 9 * outs, count_in)
    tap_flops = 2 * cells * count_in * 9 * outs

    flat = plane.reshape(cells, count_in)
    near, far = from_side(flat, 1), from_side(flat, 2)
    own_terms = vmem_call(
        functools.partial(own_plane_kernel, rows_n, cols_n),
        jax.ShapeDtypeStruct((3, cells, outs), jnp.float32),
        [flat, one_stack],
        [pltpu.VMEM((3, cells, 9 * outs), jnp.float32)],
        3 * tap_flops,
    )
    far, own_terms = lax.optimization_barrier((far, own_terms))
    their_far = from_chan_partner(far, 1)
    near, own_terms, their_far = lax.optimization_barrier((near, own_terms, their_far))
    their_near = from_chan_partner(near, 1)
    odd = (me % 2).astype(jnp.int32).reshape(1)
    hidden = vmem_call(
        functools.partial(neighbour_kernel, rows_n, cols_n),
        jax.ShapeDtypeStruct((3, cells, outs), jnp.bfloat16),
        [odd, near, far, their_near, their_far, own_terms, one_stack, bias_one.reshape(1, outs)],
        [pltpu.VMEM((3, cells, 9 * outs), jnp.float32)],
        6 * tap_flops,
        smem_first=True,
    )

    held = [(hidden[None], (0,))]
    offsets = [0]
    bit = 1
    while bit < chans:
        bit *= 2
    bit //= 2
    while bit >= 1:
        sent = jnp.stack([arr[i] for arr, offs in held for i in range(len(offs))])
        got = from_chan_partner(sent, bit)
        held.append((got, tuple(j ^ bit for j in offsets)))
        offsets = offsets + [j ^ bit for j in offsets]
        bit //= 2
    layout = tuple(offs for _, offs in held)
    me_flag = me.astype(jnp.int32).reshape(1)
    output = vmem_call(
        functools.partial(second_kernel, rows_n, cols_n, layout),
        jax.ShapeDtypeStruct((1, outs, cells), jnp.bfloat16),
        [me_flag] + [arr for arr, _ in held] + [two_stack, bias_two.reshape(1, outs)],
        [pltpu.VMEM((3, cells, count_in), jnp.bfloat16), pltpu.VMEM((1, cells, 9 * outs), jnp.float32)],
        3 * tap_flops,
        smem_first=True,
    )
    return output


def solution(mesh):
    return jax.shard_map(
        per_device,
        mesh=mesh,
        in_specs=(
            P("space", None, None, None),
            P(None, None, None, "chan", None),
            P("chan"),
            P(None, None, None, "chan", None),
            P("chan"),
        ),
        out_specs=P("space", "chan", None),
        check_vma=False,
    )
```

```python
import functools

import jax
import jax.numpy as jnp
from jax import lax
from jax.experimental import pallas as pl
from jax.experimental.pallas import tpu as pltpu
from jax.sharding import PartitionSpec as P


def gathered_from(block, source_of):
    spaces = lax.axis_size("space")
    chans = lax.axis_size("chan")
    pairs = []
    for s in range(spaces):
        for c in range(chans):
            source_s, source_c = source_of(s, c)
            pairs.append(((source_s % spaces) * chans + source_c % chans, s * chans + c))
    return lax.ppermute(block, ("space", "chan"), pairs)


def from_side(block, distance):
    return gathered_from(block, lambda s, c: (s - distance if c % 2 == 0 else s + distance, c))


def from_chan_partner(block, bit):
    return gathered_from(block, lambda s, c: (s, c ^ bit))


def spatial_sum(acc_ref, plane, rows_n, cols_n, outs):
    cells = rows_n * cols_n
    column = lax.broadcasted_iota(jnp.int32, (cells, outs), 0) % cols_n
    total = None
    for col_tap in range(3):
        shifted = None
        for row_tap in range(3):
            tap = row_tap * 3 + col_tap
            part = acc_ref[plane, :, pl.ds(tap * outs, outs)]
            amount = ((1 - row_tap) * cols_n) % cells
            if amount:
                part = pltpu.roll(part, amount, 0)
            shifted = part if shifted is None else shifted + part
        if col_tap == 0:
            shifted = jnp.where(
                column == 0,
                pltpu.roll(shifted, (1 - cols_n) % cells, 0),
                pltpu.roll(shifted, 1, 0),
            )
        elif col_tap == 2:
            shifted = jnp.where(
                column == cols_n - 1,
                pltpu.roll(shifted, cols_n - 1, 0),
                pltpu.roll(shifted, cells - 1, 0),
            )
        total = shifted if total is None else total + shifted
    return total


def tap_product(plane, w_ref, depth_tap):
    return lax.dot_general(
        plane, w_ref[depth_tap], (((1,), (1,)), ((), ())), preferred_element_type=jnp.float32
    )


def own_plane_kernel(rows_n, cols_n, x_ref, w_ref, o_ref, acc_ref):
    outs = o_ref.shape[2]
    x = x_ref[...]
    for plane in range(3):
        acc_ref[plane] = tap_product(x, w_ref, 2 - plane)
    for plane in range(3):
        o_ref[plane] = spatial_sum(acc_ref, plane, rows_n, cols_n, outs)


def neighbour_kernel(rows_n, cols_n, odd_ref, near_ref, far_ref, their_near_ref, their_far_ref, part_ref,
                     w_ref, b_ref, o_ref, acc_ref):
    outs = o_ref.shape[2]
    is_odd = odd_ref[0] != 0
    minus_one = jnp.where(is_odd, their_near_ref[...], near_ref[...])
    minus_two = jnp.where(is_odd, their_far_ref[...], far_ref[...])
    plus_one = jnp.where(is_odd, near_ref[...], their_near_ref[...])
    plus_two = jnp.where(is_odd, far_ref[...], their_far_ref[...])
    acc_ref[0] = tap_product(minus_two, w_ref, 0)
    acc_ref[1] = tap_product(minus_one, w_ref, 0)
    acc_ref[0] += tap_product(minus_one, w_ref, 1)
    acc_ref[2] = tap_product(plus_one, w_ref, 1)
    acc_ref[1] += tap_product(plus_one, w_ref, 2)
    acc_ref[2] += tap_product(plus_two, w_ref, 2)
    bias = b_ref[...]
    for plane in range(3):
        total = spatial_sum(acc_ref, plane, rows_n, cols_n, outs) + part_ref[plane]
        o_ref[plane] = jnp.maximum(total + bias, 0.0).astype(o_ref.dtype)


def second_kernel(rows_n, cols_n, layout, me_ref, *refs):
    inputs = refs[:len(layout)]
    w_ref, b_ref, o_ref, field_ref, acc_ref = refs[len(layout):]
    outs = b_ref.shape[1]
    me = me_ref[0]
    blocks = {}
    for ref, offsets in zip(inputs, layout):
        for position, j in enumerate(offsets):
            blocks[j] = ref[position]
    count = len(blocks)
    ordered = [blocks[j] for j in range(count)]
    bit = 1
    while bit < count:
        flip = (me & bit) != 0
        ordered = [jnp.where(flip, ordered[j ^ bit], ordered[j]) for j in range(count)]
        bit *= 2
    for position in range(count):
        field_ref[:, :, pl.ds(position * outs, outs)] = ordered[position]
    acc_ref[0] = tap_product(field_ref[0], w_ref, 0)
    for depth_tap in (1, 2):
        acc_ref[0] += tap_product(field_ref[depth_tap], w_ref, depth_tap)
    total = spatial_sum(acc_ref, 0, rows_n, cols_n, outs)
    result = jnp.maximum(total + b_ref[...], 0.0)
    o_ref[0] = result.T.astype(o_ref.dtype)


def vmem_call(kernel, out_shape, operands, scratch, flops, smem_first=False):
    specs = [pl.BlockSpec(memory_space=pltpu.VMEM) for _ in operands]
    if smem_first:
        specs[0] = pl.BlockSpec(memory_space=pltpu.SMEM)
    moved = sum(x.size * x.dtype.itemsize for x in operands) + out_shape.size * out_shape.dtype.itemsize
    return pl.pallas_call(
        kernel,
        out_shape=out_shape,
        in_specs=specs,
        out_specs=pl.BlockSpec(memory_space=pltpu.VMEM),
        scratch_shapes=scratch,
        compiler_params=pltpu.CompilerParams(vmem_limit_bytes=48 * 1024 * 1024),
        cost_estimate=pl.CostEstimate(flops=flops, transcendentals=0, bytes_accessed=moved),
    )(*operands)


def per_device(volume, weight_one, bias_one, weight_two, bias_two):
    plane = volume[0]
    rows_n, cols_n, count_in = plane.shape
    cells = rows_n * cols_n
    outs = weight_one.shape[3]
    me = lax.axis_index("chan")
    chans = lax.axis_size("chan")
    one_stack = weight_one.reshape(3, 9 * outs, count_in)
    two_stack = weight_two.reshape(3, 9 * outs, count_in)
    tap_flops = 2 * cells * count_in * 9 * outs

    flat = plane.reshape(cells, count_in)
    near, far = from_side(flat, 1), from_side(flat, 2)
    own_terms = vmem_call(
        functools.partial(own_plane_kernel, rows_n, cols_n),
        jax.ShapeDtypeStruct((3, cells, outs), jnp.float32),
        [flat, one_stack],
        [pltpu.VMEM((3, cells, 9 * outs), jnp.float32)],
        3 * tap_flops,
    )
    near, far, own_terms = lax.optimization_barrier((near, far, own_terms))
    their_near, their_far = from_chan_partner(near, 1), from_chan_partner(far, 1)
    odd = (me % 2).astype(jnp.int32).reshape(1)
    hidden = vmem_call(
        functools.partial(neighbour_kernel, rows_n, cols_n),
        jax.ShapeDtypeStruct((3, cells, outs), jnp.bfloat16),
        [odd, near, far, their_near, their_far, own_terms, one_stack, bias_one.reshape(1, outs)],
        [pltpu.VMEM((3, cells, 9 * outs), jnp.float32)],
        6 * tap_flops,
        smem_first=True,
    )

    held = [(hidden[None], (0,))]
    offsets = [0]
    bit = 1
    while bit < chans:
        bit *= 2
    bit //= 2
    while bit >= 1:
        sent = jnp.stack([arr[i] for arr, offs in held for i in range(len(offs))])
        got = from_chan_partner(sent, bit)
        held.append((got, tuple(j ^ bit for j in offsets)))
        offsets = offsets + [j ^ bit for j in offsets]
        bit //= 2
    layout = tuple(offs for _, offs in held)
    me_flag = me.astype(jnp.int32).reshape(1)
    output = vmem_call(
        functools.partial(second_kernel, rows_n, cols_n, layout),
        jax.ShapeDtypeStruct((1, outs, cells), jnp.bfloat16),
        [me_flag] + [arr for arr, _ in held] + [two_stack, bias_two.reshape(1, outs)],
        [pltpu.VMEM((3, cells, count_in), jnp.bfloat16), pltpu.VMEM((1, cells, 9 * outs), jnp.float32)],
        3 * tap_flops,
        smem_first=True,
    )
    return output


def solution(mesh):
    return jax.shard_map(
        per_device,
        mesh=mesh,
        in_specs=(
            P("space", None, None, None),
            P(None, None, None, "chan", None),
            P("chan"),
            P(None, None, None, "chan", None),
            P("chan"),
        ),
        out_specs=P("space", "chan", None),
        check_vma=False,
    )
```

```python
import functools

import jax
import jax.numpy as jnp
from jax import lax
from jax.experimental import pallas as pl
from jax.experimental.pallas import tpu as pltpu
from jax.sharding import PartitionSpec as P


def gathered_from(block, source_of):
    spaces = lax.axis_size("space")
    chans = lax.axis_size("chan")
    pairs = []
    for s in range(spaces):
        for c in range(chans):
            source_s, source_c = source_of(s, c)
            pairs.append(((source_s % spaces) * chans + source_c % chans, s * chans + c))
    return lax.ppermute(block, ("space", "chan"), pairs)


def from_side(block, distance):
    return gathered_from(block, lambda s, c: (s - distance if c % 2 == 0 else s + distance, c))


def from_chan_partner(block, bit):
    return gathered_from(block, lambda s, c: (s, c ^ bit))


def spatial_sum(acc_ref, plane, rows_n, cols_n, outs):
    cells = rows_n * cols_n
    column = lax.broadcasted_iota(jnp.int32, (cells, outs), 0) % cols_n
    total = None
    for col_tap in range(3):
        shifted = None
        for row_tap in range(3):
            tap = row_tap * 3 + col_tap
            if len(acc_ref.shape) == 3:
                part = acc_ref[plane, :, pl.ds(tap * outs, outs)]
            else:
                part = acc_ref[pl.ds(plane * cells, cells), pl.ds(tap * outs, outs)]
            amount = ((1 - row_tap) * cols_n) % cells
            if amount:
                part = pltpu.roll(part, amount, 0)
            shifted = part if shifted is None else shifted + part
        if col_tap == 0:
            shifted = jnp.where(
                column == 0,
                pltpu.roll(shifted, (1 - cols_n) % cells, 0),
                pltpu.roll(shifted, 1, 0),
            )
        elif col_tap == 2:
            shifted = jnp.where(
                column == cols_n - 1,
                pltpu.roll(shifted, cols_n - 1, 0),
                pltpu.roll(shifted, cells - 1, 0),
            )
        total = shifted if total is None else total + shifted
    return total


def tap_product(plane, w_ref, depth_tap):
    return lax.dot_general(
        plane, w_ref[depth_tap], (((1,), (1,)), ((), ())), preferred_element_type=jnp.float32
    )


def own_plane_kernel(rows_n, cols_n, x_ref, w_ref, o_ref, acc_ref):
    outs = o_ref.shape[2]
    x = x_ref[...]
    for index, depth_tap in enumerate((2, 0)):
        acc_ref[index] = tap_product(x, w_ref, depth_tap)
    for index in range(2):
        o_ref[index] = spatial_sum(acc_ref, index, rows_n, cols_n, outs)


def neighbour_kernel(rows_n, cols_n, odd_ref, own_ref, near_ref, far_ref, their_near_ref, their_far_ref,
                     part_ref, w_ref, b_ref, o_ref, field_ref, acc_ref):
    outs = o_ref.shape[2]
    cells = rows_n * cols_n
    is_odd = odd_ref[0] != 0
    field_ref[pl.ds(0, cells)] = jnp.where(is_odd, their_far_ref[...], far_ref[...])
    field_ref[pl.ds(cells, cells)] = jnp.where(is_odd, their_near_ref[...], near_ref[...])
    field_ref[pl.ds(2 * cells, cells)] = own_ref[...]
    field_ref[pl.ds(3 * cells, cells)] = jnp.where(is_odd, near_ref[...], their_near_ref[...])
    field_ref[pl.ds(4 * cells, cells)] = jnp.where(is_odd, far_ref[...], their_far_ref[...])
    acc_ref[pl.ds(0, 2 * cells)] = tap_product(field_ref[pl.ds(0, 2 * cells)], w_ref, 0)
    upper = tap_product(field_ref[pl.ds(3 * cells, 2 * cells)], w_ref, 2)
    acc_ref[pl.ds(2 * cells, cells)] = upper[cells:]
    acc_ref[pl.ds(cells, cells)] += upper[:cells]
    acc_ref[...] += tap_product(field_ref[pl.ds(cells, 3 * cells)], w_ref, 1)
    bias = b_ref[...]
    for plane in range(3):
        total = spatial_sum(acc_ref, plane, rows_n, cols_n, outs)
        if plane != 1:
            total = total + part_ref[plane // 2]
        o_ref[plane] = jnp.maximum(total + bias, 0.0).astype(o_ref.dtype)


def second_kernel(rows_n, cols_n, layout, me_ref, *refs):
    inputs = refs[:len(layout)]
    w_ref, b_ref, o_ref, field_ref, acc_ref = refs[len(layout):]
    outs = b_ref.shape[1]
    me = me_ref[0]
    blocks = {}
    for ref, offsets in zip(inputs, layout):
        for position, j in enumerate(offsets):
            blocks[j] = ref[position]
    count = len(blocks)
    ordered = [blocks[j] for j in range(count)]
    bit = 1
    while bit < count:
        flip = (me & bit) != 0
        ordered = [jnp.where(flip, ordered[j ^ bit], ordered[j]) for j in range(count)]
        bit *= 2
    for position in range(count):
        field_ref[:, :, pl.ds(position * outs, outs)] = ordered[position]
    acc_ref[0] = tap_product(field_ref[0], w_ref, 0)
    for depth_tap in (1, 2):
        acc_ref[0] += tap_product(field_ref[depth_tap], w_ref, depth_tap)
    total = spatial_sum(acc_ref, 0, rows_n, cols_n, outs)
    result = jnp.maximum(total + b_ref[...], 0.0)
    o_ref[0] = result.T.astype(o_ref.dtype)


def vmem_call(kernel, out_shape, operands, scratch, flops, smem_first=False):
    specs = [pl.BlockSpec(memory_space=pltpu.VMEM) for _ in operands]
    if smem_first:
        specs[0] = pl.BlockSpec(memory_space=pltpu.SMEM)
    moved = sum(x.size * x.dtype.itemsize for x in operands) + out_shape.size * out_shape.dtype.itemsize
    return pl.pallas_call(
        kernel,
        out_shape=out_shape,
        in_specs=specs,
        out_specs=pl.BlockSpec(memory_space=pltpu.VMEM),
        scratch_shapes=scratch,
        compiler_params=pltpu.CompilerParams(vmem_limit_bytes=48 * 1024 * 1024),
        cost_estimate=pl.CostEstimate(flops=flops, transcendentals=0, bytes_accessed=moved),
    )(*operands)


def per_device(volume, weight_one, bias_one, weight_two, bias_two):
    plane = volume[0]
    rows_n, cols_n, count_in = plane.shape
    cells = rows_n * cols_n
    outs = weight_one.shape[3]
    me = lax.axis_index("chan")
    chans = lax.axis_size("chan")
    one_stack = weight_one.reshape(3, 9 * outs, count_in)
    two_stack = weight_two.reshape(3, 9 * outs, count_in)
    tap_flops = 2 * cells * count_in * 9 * outs

    flat = plane.reshape(cells, count_in)
    near, far = from_side(flat, 1), from_side(flat, 2)
    own_terms = vmem_call(
        functools.partial(own_plane_kernel, rows_n, cols_n),
        jax.ShapeDtypeStruct((2, cells, outs), jnp.float32),
        [flat, one_stack],
        [pltpu.VMEM((2, cells, 9 * outs), jnp.float32)],
        2 * tap_flops,
    )
    near, far, own_terms = lax.optimization_barrier((near, far, own_terms))
    their_near, their_far = from_chan_partner(near, 1), from_chan_partner(far, 1)
    odd = (me % 2).astype(jnp.int32).reshape(1)
    hidden = vmem_call(
        functools.partial(neighbour_kernel, rows_n, cols_n),
        jax.ShapeDtypeStruct((3, cells, outs), jnp.bfloat16),
        [odd, flat, near, far, their_near, their_far, own_terms, one_stack, bias_one.reshape(1, outs)],
        [pltpu.VMEM((5 * cells, count_in), jnp.bfloat16), pltpu.VMEM((3 * cells, 9 * outs), jnp.float32)],
        7 * tap_flops,
        smem_first=True,
    )

    held = [(hidden[None], (0,))]
    offsets = [0]
    bit = 1
    while bit < chans:
        bit *= 2
    bit //= 2
    while bit >= 1:
        sent = jnp.stack([arr[i] for arr, offs in held for i in range(len(offs))])
        got = from_chan_partner(sent, bit)
        held.append((got, tuple(j ^ bit for j in offsets)))
        offsets = offsets + [j ^ bit for j in offsets]
        bit //= 2
    layout = tuple(offs for _, offs in held)
    me_flag = me.astype(jnp.int32).reshape(1)
    output = vmem_call(
        functools.partial(second_kernel, rows_n, cols_n, layout),
        jax.ShapeDtypeStruct((1, outs, cells), jnp.bfloat16),
        [me_flag] + [arr for arr, _ in held] + [two_stack, bias_two.reshape(1, outs)],
        [pltpu.VMEM((3, cells, count_in), jnp.bfloat16), pltpu.VMEM((1, cells, 9 * outs), jnp.float32)],
        3 * tap_flops,
        smem_first=True,
    )
    return output


def solution(mesh):
    return jax.shard_map(
        per_device,
        mesh=mesh,
        in_specs=(
            P("space", None, None, None),
            P(None, None, None, "chan", None),
            P("chan"),
            P(None, None, None, "chan", None),
            P("chan"),
        ),
        out_specs=P("space", "chan", None),
        check_vma=False,
    )
```

```python
import functools

import jax
import jax.numpy as jnp
from jax import lax
from jax.experimental import pallas as pl
from jax.experimental.pallas import tpu as pltpu
from jax.sharding import PartitionSpec as P


def gathered_from(block, source_of):
    spaces = lax.axis_size("space")
    chans = lax.axis_size("chan")
    pairs = []
    for s in range(spaces):
        for c in range(chans):
            source_s, source_c = source_of(s, c)
            pairs.append(((source_s % spaces) * chans + source_c % chans, s * chans + c))
    return lax.ppermute(block, ("space", "chan"), pairs)


def from_side(block, distance):
    return gathered_from(block, lambda s, c: (s - distance if c % 2 == 0 else s + distance, c))


def from_chan_partner(block, bit):
    return gathered_from(block, lambda s, c: (s, c ^ bit))


def spatial_sum(acc_ref, plane, rows_n, cols_n, outs):
    cells = rows_n * cols_n
    column = lax.broadcasted_iota(jnp.int32, (cells, outs), 0) % cols_n
    total = None
    for col_tap in range(3):
        shifted = None
        for row_tap in range(3):
            tap = row_tap * 3 + col_tap
            part = acc_ref[plane, :, pl.ds(tap * outs, outs)]
            amount = ((1 - row_tap) * cols_n) % cells
            if amount:
                part = pltpu.roll(part, amount, 0)
            shifted = part if shifted is None else shifted + part
        if col_tap == 0:
            shifted = jnp.where(
                column == 0,
                pltpu.roll(shifted, (1 - cols_n) % cells, 0),
                pltpu.roll(shifted, 1, 0),
            )
        elif col_tap == 2:
            shifted = jnp.where(
                column == cols_n - 1,
                pltpu.roll(shifted, cols_n - 1, 0),
                pltpu.roll(shifted, cells - 1, 0),
            )
        total = shifted if total is None else total + shifted
    return total


def tap_product(plane, w_ref, depth_tap):
    return lax.dot_general(
        plane, w_ref[depth_tap], (((1,), (1,)), ((), ())), preferred_element_type=jnp.float32
    )


def own_plane_kernel(rows_n, cols_n, x_ref, w_ref, o_ref, acc_ref):
    outs = o_ref.shape[2]
    x = x_ref[...]
    for plane in range(3):
        acc_ref[plane] = tap_product(x, w_ref, 2 - plane)
    for plane in range(3):
        o_ref[plane] = spatial_sum(acc_ref, plane, rows_n, cols_n, outs)


def neighbour_kernel(rows_n, cols_n, odd_ref, near_ref, far_ref, their_near_ref, their_far_ref, part_ref,
                     w_ref, b_ref, o_ref, acc_ref):
    outs = o_ref.shape[2]
    is_odd = odd_ref[0] != 0
    minus_one = jnp.where(is_odd, their_near_ref[...], near_ref[...])
    minus_two = jnp.where(is_odd, their_far_ref[...], far_ref[...])
    plus_one = jnp.where(is_odd, near_ref[...], their_near_ref[...])
    plus_two = jnp.where(is_odd, far_ref[...], their_far_ref[...])
    acc_ref[0] = tap_product(minus_two, w_ref, 0) + tap_product(minus_one, w_ref, 1)
    acc_ref[1] = tap_product(minus_one, w_ref, 0) + tap_product(plus_one, w_ref, 2)
    acc_ref[2] = tap_product(plus_one, w_ref, 1) + tap_product(plus_two, w_ref, 2)
    bias = b_ref[...]
    for plane in range(3):
        total = spatial_sum(acc_ref, plane, rows_n, cols_n, outs) + part_ref[plane]
        o_ref[plane] = jnp.maximum(total + bias, 0.0).astype(o_ref.dtype)


def second_kernel(rows_n, cols_n, layout, me_ref, *refs):
    inputs = refs[:len(layout)]
    w_ref, b_ref, o_ref, field_ref, acc_ref = refs[len(layout):]
    outs = b_ref.shape[1]
    me = me_ref[0]
    blocks = {}
    for ref, offsets in zip(inputs, layout):
        for position, j in enumerate(offsets):
            blocks[j] = ref[position]
    count = len(blocks)
    ordered = [blocks[j] for j in range(count)]
    bit = 1
    while bit < count:
        flip = (me & bit) != 0
        ordered = [jnp.where(flip, ordered[j ^ bit], ordered[j]) for j in range(count)]
        bit *= 2
    for position in range(count):
        field_ref[:, :, pl.ds(position * outs, outs)] = ordered[position]
    products = None
    for depth_tap in range(3):
        term = tap_product(field_ref[depth_tap], w_ref, depth_tap)
        products = term if products is None else products + term
    acc_ref[0] = products
    total = spatial_sum(acc_ref, 0, rows_n, cols_n, outs)
    result = jnp.maximum(total + b_ref[...], 0.0)
    o_ref[0] = result.T.astype(o_ref.dtype)


def vmem_call(kernel, out_shape, operands, scratch, flops, smem_first=False):
    specs = [pl.BlockSpec(memory_space=pltpu.VMEM) for _ in operands]
    if smem_first:
        specs[0] = pl.BlockSpec(memory_space=pltpu.SMEM)
    moved = sum(x.size * x.dtype.itemsize for x in operands) + out_shape.size * out_shape.dtype.itemsize
    return pl.pallas_call(
        kernel,
        out_shape=out_shape,
        in_specs=specs,
        out_specs=pl.BlockSpec(memory_space=pltpu.VMEM),
        scratch_shapes=scratch,
        compiler_params=pltpu.CompilerParams(vmem_limit_bytes=48 * 1024 * 1024),
        cost_estimate=pl.CostEstimate(flops=flops, transcendentals=0, bytes_accessed=moved),
    )(*operands)


def per_device(volume, weight_one, bias_one, weight_two, bias_two):
    plane = volume[0]
    rows_n, cols_n, count_in = plane.shape
    cells = rows_n * cols_n
    outs = weight_one.shape[3]
    me = lax.axis_index("chan")
    chans = lax.axis_size("chan")
    one_stack = weight_one.reshape(3, 9 * outs, count_in)
    two_stack = weight_two.reshape(3, 9 * outs, count_in)
    tap_flops = 2 * cells * count_in * 9 * outs

    flat = plane.reshape(cells, count_in)
    near, far = from_side(flat, 1), from_side(flat, 2)
    own_terms = vmem_call(
        functools.partial(own_plane_kernel, rows_n, cols_n),
        jax.ShapeDtypeStruct((3, cells, outs), jnp.float32),
        [flat, one_stack],
        [pltpu.VMEM((3, cells, 9 * outs), jnp.float32)],
        3 * tap_flops,
    )
    near, far, own_terms = lax.optimization_barrier((near, far, own_terms))
    their_near, their_far = from_chan_partner(near, 1), from_chan_partner(far, 1)
    odd = (me % 2).astype(jnp.int32).reshape(1)
    hidden = vmem_call(
        functools.partial(neighbour_kernel, rows_n, cols_n),
        jax.ShapeDtypeStruct((3, cells, outs), jnp.bfloat16),
        [odd, near, far, their_near, their_far, own_terms, one_stack, bias_one.reshape(1, outs)],
        [pltpu.VMEM((3, cells, 9 * outs), jnp.float32)],
        6 * tap_flops,
        smem_first=True,
    )

    held = [(hidden[None], (0,)), (from_chan_partner(hidden, 1)[None], (1,))]
    remote = [(hidden[None], (0,))]
    offsets = [0]
    bit = 2
    while bit < chans:
        sent = jnp.stack([arr[i] for arr, offs in remote for i in range(len(offs))])
        got = from_chan_partner(sent, bit)
        remote.append((got, tuple(j ^ bit for j in offsets)))
        offsets = offsets + [j ^ bit for j in offsets]
        bit *= 2
    if len(remote) > 1:
        received = [(arr, offs) for arr, offs in remote[1:]]
        held.extend(received)
        sent = jnp.stack([arr[i] for arr, offs in received for i in range(len(offs))])
        forwarded = from_chan_partner(sent, 1)
        held.append((forwarded, tuple(j ^ 1 for _, offs in received for j in offs)))
    layout = tuple(offs for _, offs in held)
    me_flag = me.astype(jnp.int32).reshape(1)
    output = vmem_call(
        functools.partial(second_kernel, rows_n, cols_n, layout),
        jax.ShapeDtypeStruct((1, outs, cells), jnp.bfloat16),
        [me_flag] + [arr for arr, _ in held] + [two_stack, bias_two.reshape(1, outs)],
        [pltpu.VMEM((3, cells, count_in), jnp.bfloat16), pltpu.VMEM((1, cells, 9 * outs), jnp.float32)],
        3 * tap_flops,
        smem_first=True,
    )
    return output


def solution(mesh):
    return jax.shard_map(
        per_device,
        mesh=mesh,
        in_specs=(
            P("space", None, None, None),
            P(None, None, None, "chan", None),
            P("chan"),
            P(None, None, None, "chan", None),
            P("chan"),
        ),
        out_specs=P("space", "chan", None),
        check_vma=False,
    )
```

```python
import functools

import jax
import jax.numpy as jnp
from jax import lax
from jax.experimental import pallas as pl
from jax.experimental.pallas import tpu as pltpu
from jax.sharding import PartitionSpec as P


def gathered_from(block, source_of):
    spaces = lax.axis_size("space")
    chans = lax.axis_size("chan")
    pairs = []
    for s in range(spaces):
        for c in range(chans):
            source_s, source_c = source_of(s, c)
            pairs.append(((source_s % spaces) * chans + source_c % chans, s * chans + c))
    return lax.ppermute(block, ("space", "chan"), pairs)


def from_side(block, distance):
    return gathered_from(block, lambda s, c: (s - distance if c % 2 == 0 else s + distance, c))


def from_chan_partner(block, bit):
    return gathered_from(block, lambda s, c: (s, c ^ bit))


def spatial_sum(acc_ref, plane, rows_n, cols_n, outs):
    cells = rows_n * cols_n
    column = lax.broadcasted_iota(jnp.int32, (cells, outs), 0) % cols_n
    total = None
    for col_tap in range(3):
        shifted = None
        for row_tap in range(3):
            tap = row_tap * 3 + col_tap
            part = acc_ref[plane, :, pl.ds(tap * outs, outs)]
            amount = ((1 - row_tap) * cols_n) % cells
            if amount:
                part = pltpu.roll(part, amount, 0)
            shifted = part if shifted is None else shifted + part
        if col_tap == 0:
            shifted = jnp.where(
                column == 0,
                pltpu.roll(shifted, (1 - cols_n) % cells, 0),
                pltpu.roll(shifted, 1, 0),
            )
        elif col_tap == 2:
            shifted = jnp.where(
                column == cols_n - 1,
                pltpu.roll(shifted, cols_n - 1, 0),
                pltpu.roll(shifted, cells - 1, 0),
            )
        total = shifted if total is None else total + shifted
    return total


def tap_product(plane, w_ref, depth_tap):
    return lax.dot_general(
        plane, w_ref[depth_tap], (((1,), (1,)), ((), ())), preferred_element_type=jnp.float32
    )


def own_plane_kernel(rows_n, cols_n, x_ref, w_ref, o_ref, send_ref, acc_ref):
    outs = o_ref.shape[2]
    x = x_ref[...]
    for plane in range(3):
        acc_ref[plane] = tap_product(x, w_ref, 2 - plane)
    for plane in range(3):
        terms = spatial_sum(acc_ref, plane, rows_n, cols_n, outs)
        o_ref[plane] = terms
        if plane != 1:
            send_ref[plane // 2] = terms


def neighbour_kernel(rows_n, cols_n, odd_ref, near_ref, their_near_ref, below_ref, above_ref, part_ref,
                     w_ref, b_ref, o_ref, acc_ref):
    outs = o_ref.shape[2]
    is_odd = odd_ref[0] != 0
    minus_one = jnp.where(is_odd, their_near_ref[...], near_ref[...])
    plus_one = jnp.where(is_odd, near_ref[...], their_near_ref[...])
    acc_ref[0] = tap_product(minus_one, w_ref, 1)
    acc_ref[1] = tap_product(minus_one, w_ref, 0)
    acc_ref[1] += tap_product(plus_one, w_ref, 2)
    acc_ref[2] = tap_product(plus_one, w_ref, 1)
    bias = b_ref[...]
    far = {0: below_ref, 2: above_ref}
    for plane in range(3):
        total = spatial_sum(acc_ref, plane, rows_n, cols_n, outs) + part_ref[plane]
        if plane in far:
            total = total + far[plane][...]
        o_ref[plane] = jnp.maximum(total + bias, 0.0).astype(o_ref.dtype)


def second_kernel(rows_n, cols_n, layout, me_ref, *refs):
    inputs = refs[:len(layout)]
    w_ref, b_ref, o_ref, field_ref, acc_ref = refs[len(layout):]
    outs = b_ref.shape[1]
    me = me_ref[0]
    blocks = {}
    for ref, offsets in zip(inputs, layout):
        for position, j in enumerate(offsets):
            blocks[j] = ref[position]
    count = len(blocks)
    ordered = [blocks[j] for j in range(count)]
    bit = 1
    while bit < count:
        flip = (me & bit) != 0
        ordered = [jnp.where(flip, ordered[j ^ bit], ordered[j]) for j in range(count)]
        bit *= 2
    for position in range(count):
        field_ref[:, :, pl.ds(position * outs, outs)] = ordered[position]
    products = None
    for depth_tap in range(3):
        term = tap_product(field_ref[depth_tap], w_ref, depth_tap)
        products = term if products is None else products + term
    acc_ref[0] = products
    total = spatial_sum(acc_ref, 0, rows_n, cols_n, outs)
    result = jnp.maximum(total + b_ref[...], 0.0)
    o_ref[0] = result.T.astype(o_ref.dtype)


def vmem_call(kernel, out_shape, operands, scratch, flops, smem_first=False):
    specs = [pl.BlockSpec(memory_space=pltpu.VMEM) for _ in operands]
    if smem_first:
        specs[0] = pl.BlockSpec(memory_space=pltpu.SMEM)
    outs_list = out_shape if isinstance(out_shape, tuple) else (out_shape,)
    moved = sum(x.size * x.dtype.itemsize for x in operands) + sum(o.size * o.dtype.itemsize for o in outs_list)
    return pl.pallas_call(
        kernel,
        out_shape=out_shape,
        in_specs=specs,
        out_specs=tuple(pl.BlockSpec(memory_space=pltpu.VMEM) for _ in outs_list)
        if isinstance(out_shape, tuple) else pl.BlockSpec(memory_space=pltpu.VMEM),
        scratch_shapes=scratch,
        compiler_params=pltpu.CompilerParams(vmem_limit_bytes=48 * 1024 * 1024),
        cost_estimate=pl.CostEstimate(flops=flops, transcendentals=0, bytes_accessed=moved),
    )(*operands)


def per_device(volume, weight_one, bias_one, weight_two, bias_two):
    plane = volume[0]
    rows_n, cols_n, count_in = plane.shape
    cells = rows_n * cols_n
    outs = weight_one.shape[3]
    me = lax.axis_index("chan")
    chans = lax.axis_size("chan")
    one_stack = weight_one.reshape(3, 9 * outs, count_in)
    two_stack = weight_two.reshape(3, 9 * outs, count_in)
    tap_flops = 2 * cells * count_in * 9 * outs

    flat = plane.reshape(cells, count_in)
    near = from_side(flat, 1)
    own_terms, sent = vmem_call(
        functools.partial(own_plane_kernel, rows_n, cols_n),
        (jax.ShapeDtypeStruct((3, cells, outs), jnp.float32), jax.ShapeDtypeStruct((2, cells, outs), jnp.float32)),
        [flat, one_stack],
        [pltpu.VMEM((3, cells, 9 * outs), jnp.float32)],
        3 * tap_flops,
    )
    below = gathered_from(sent[1], lambda s, c: (s - 2, c))
    above = gathered_from(sent[0], lambda s, c: (s + 2, c))
    near, below, above = lax.optimization_barrier((near, below, above))
    their_near = from_chan_partner(near, 1)
    odd = (me % 2).astype(jnp.int32).reshape(1)
    hidden = vmem_call(
        functools.partial(neighbour_kernel, rows_n, cols_n),
        jax.ShapeDtypeStruct((3, cells, outs), jnp.bfloat16),
        [odd, near, their_near, below, above, own_terms, one_stack, bias_one.reshape(1, outs)],
        [pltpu.VMEM((3, cells, 9 * outs), jnp.float32)],
        4 * tap_flops,
        smem_first=True,
    )

    held = [(hidden[None], (0,))]
    offsets = [0]
    bit = 1
    while bit < chans:
        bit *= 2
    bit //= 2
    while bit >= 1:
        sent = jnp.stack([arr[i] for arr, offs in held for i in range(len(offs))])
        got = from_chan_partner(sent, bit)
        held.append((got, tuple(j ^ bit for j in offsets)))
        offsets = offsets + [j ^ bit for j in offsets]
        bit //= 2
    layout = tuple(offs for _, offs in held)
    me_flag = me.astype(jnp.int32).reshape(1)
    output = vmem_call(
        functools.partial(second_kernel, rows_n, cols_n, layout),
        jax.ShapeDtypeStruct((1, outs, cells), jnp.bfloat16),
        [me_flag] + [arr for arr, _ in held] + [two_stack, bias_two.reshape(1, outs)],
        [pltpu.VMEM((3, cells, count_in), jnp.bfloat16), pltpu.VMEM((1, cells, 9 * outs), jnp.float32)],
        3 * tap_flops,
        smem_first=True,
    )
    return output


def solution(mesh):
    return jax.shard_map(
        per_device,
        mesh=mesh,
        in_specs=(
            P("space", None, None, None),
            P(None, None, None, "chan", None),
            P("chan"),
            P(None, None, None, "chan", None),
            P("chan"),
        ),
        out_specs=P("space", "chan", None),
        check_vma=False,
    )
```

```python
import functools

import jax
import jax.numpy as jnp
from jax import lax
from jax.experimental import pallas as pl
from jax.experimental.pallas import tpu as pltpu
from jax.sharding import PartitionSpec as P


def gathered_from(block, source_of):
    spaces = lax.axis_size("space")
    chans = lax.axis_size("chan")
    pairs = []
    for s in range(spaces):
        for c in range(chans):
            source_s, source_c = source_of(s, c)
            pairs.append(((source_s % spaces) * chans + source_c % chans, s * chans + c))
    return lax.ppermute(block, ("space", "chan"), pairs)


def from_side(block, distance):
    return gathered_from(block, lambda s, c: (s - distance if c % 2 == 0 else s + distance, c))


def from_chan_partner(block, bit):
    return gathered_from(block, lambda s, c: (s, c ^ bit))


def spatial_sum(acc_ref, plane, rows_n, cols_n, outs):
    cells = rows_n * cols_n
    column = lax.broadcasted_iota(jnp.int32, (cells, outs), 0) % cols_n
    total = None
    for col_tap in range(3):
        shifted = None
        for row_tap in range(3):
            tap = row_tap * 3 + col_tap
            part = acc_ref[plane, :, pl.ds(tap * outs, outs)]
            amount = ((1 - row_tap) * cols_n) % cells
            if amount:
                part = pltpu.roll(part, amount, 0)
            shifted = part if shifted is None else shifted + part
        if col_tap == 0:
            shifted = jnp.where(
                column == 0,
                pltpu.roll(shifted, (1 - cols_n) % cells, 0),
                pltpu.roll(shifted, 1, 0),
            )
        elif col_tap == 2:
            shifted = jnp.where(
                column == cols_n - 1,
                pltpu.roll(shifted, cols_n - 1, 0),
                pltpu.roll(shifted, cells - 1, 0),
            )
        total = shifted if total is None else total + shifted
    return total


def tap_product(plane, w_ref, depth_tap):
    return lax.dot_general(
        plane, w_ref[depth_tap], (((1,), (1,)), ((), ())), preferred_element_type=jnp.float32
    )


def own_plane_kernel(rows_n, cols_n, x_ref, w_ref, o_ref, acc_ref):
    outs = o_ref.shape[2]
    x = x_ref[...]
    for plane in range(3):
        acc_ref[plane] = tap_product(x, w_ref, 2 - plane)
    for plane in range(3):
        o_ref[plane] = spatial_sum(acc_ref, plane, rows_n, cols_n, outs)


def side_products(acc_ref, first_ref, second_ref, w_ref, minus):
    if minus:
        acc_ref[0] = tap_product(second_ref[...], w_ref, 0)
        acc_ref[0] += tap_product(first_ref[...], w_ref, 1)
        acc_ref[1] = tap_product(first_ref[...], w_ref, 0)
        return (0, 1)
    acc_ref[1] = tap_product(first_ref[...], w_ref, 2)
    acc_ref[2] = tap_product(first_ref[...], w_ref, 1)
    acc_ref[2] += tap_product(second_ref[...], w_ref, 2)
    return (1, 2)


def fetched_side_kernel(rows_n, cols_n, odd_ref, near_ref, far_ref, w_ref, o_ref, acc_ref):
    outs = o_ref.shape[2]
    for minus in (True, False):

        @pl.when((odd_ref[0] == 0) == minus)
        def _():
            touched = side_products(acc_ref, near_ref, far_ref, w_ref, minus)
            for plane in range(3):
                if plane in touched:
                    o_ref[plane] = spatial_sum(acc_ref, plane, rows_n, cols_n, outs)
                else:
                    o_ref[plane] = jnp.zeros(o_ref.shape[1:], o_ref.dtype)


def neighbour_kernel(rows_n, cols_n, odd_ref, their_near_ref, their_far_ref, fetched_ref, part_ref,
                     w_ref, b_ref, o_ref, acc_ref):
    outs = o_ref.shape[2]
    bias = b_ref[...]
    for minus in (True, False):

        @pl.when((odd_ref[0] != 0) == minus)
        def _():
            touched = side_products(acc_ref, their_near_ref, their_far_ref, w_ref, minus)
            for plane in range(3):
                total = fetched_ref[plane] + part_ref[plane]
                if plane in touched:
                    total = total + spatial_sum(acc_ref, plane, rows_n, cols_n, outs)
                o_ref[plane] = jnp.maximum(total + bias, 0.0).astype(o_ref.dtype)


def second_kernel(rows_n, cols_n, layout, me_ref, *refs):
    inputs = refs[:len(layout)]
    w_ref, b_ref, o_ref, field_ref, acc_ref = refs[len(layout):]
    outs = b_ref.shape[1]
    me = me_ref[0]
    blocks = {}
    for ref, offsets in zip(inputs, layout):
        for position, j in enumerate(offsets):
            blocks[j] = ref[position]
    count = len(blocks)
    ordered = [blocks[j] for j in range(count)]
    bit = 1
    while bit < count:
        flip = (me & bit) != 0
        ordered = [jnp.where(flip, ordered[j ^ bit], ordered[j]) for j in range(count)]
        bit *= 2
    for position in range(count):
        field_ref[:, :, pl.ds(position * outs, outs)] = ordered[position]
    products = None
    for depth_tap in range(3):
        term = tap_product(field_ref[depth_tap], w_ref, depth_tap)
        products = term if products is None else products + term
    acc_ref[0] = products
    total = spatial_sum(acc_ref, 0, rows_n, cols_n, outs)
    result = jnp.maximum(total + b_ref[...], 0.0)
    o_ref[0] = result.T.astype(o_ref.dtype)


def vmem_call(kernel, out_shape, operands, scratch, flops, smem_first=False):
    specs = [pl.BlockSpec(memory_space=pltpu.VMEM) for _ in operands]
    if smem_first:
        specs[0] = pl.BlockSpec(memory_space=pltpu.SMEM)
    moved = sum(x.size * x.dtype.itemsize for x in operands) + out_shape.size * out_shape.dtype.itemsize
    return pl.pallas_call(
        kernel,
        out_shape=out_shape,
        in_specs=specs,
        out_specs=pl.BlockSpec(memory_space=pltpu.VMEM),
        scratch_shapes=scratch,
        compiler_params=pltpu.CompilerParams(vmem_limit_bytes=48 * 1024 * 1024),
        cost_estimate=pl.CostEstimate(flops=flops, transcendentals=0, bytes_accessed=moved),
    )(*operands)


def per_device(volume, weight_one, bias_one, weight_two, bias_two):
    plane = volume[0]
    rows_n, cols_n, count_in = plane.shape
    cells = rows_n * cols_n
    outs = weight_one.shape[3]
    me = lax.axis_index("chan")
    chans = lax.axis_size("chan")
    one_stack = weight_one.reshape(3, 9 * outs, count_in)
    two_stack = weight_two.reshape(3, 9 * outs, count_in)
    tap_flops = 2 * cells * count_in * 9 * outs

    flat = plane.reshape(cells, count_in)
    near, far = from_side(flat, 1), from_side(flat, 2)
    own_terms = vmem_call(
        functools.partial(own_plane_kernel, rows_n, cols_n),
        jax.ShapeDtypeStruct((3, cells, outs), jnp.float32),
        [flat, one_stack],
        [pltpu.VMEM((3, cells, 9 * outs), jnp.float32)],
        3 * tap_flops,
    )
    near, far, own_terms = lax.optimization_barrier((near, far, own_terms))
    their_near, their_far = from_chan_partner(near, 1), from_chan_partner(far, 1)
    odd = (me % 2).astype(jnp.int32).reshape(1)
    fetched_terms = vmem_call(
        functools.partial(fetched_side_kernel, rows_n, cols_n),
        jax.ShapeDtypeStruct((3, cells, outs), jnp.float32),
        [odd, near, far, one_stack],
        [pltpu.VMEM((3, cells, 9 * outs), jnp.float32)],
        3 * tap_flops,
        smem_first=True,
    )
    hidden = vmem_call(
        functools.partial(neighbour_kernel, rows_n, cols_n),
        jax.ShapeDtypeStruct((3, cells, outs), jnp.bfloat16),
        [odd, their_near, their_far, fetched_terms, own_terms, one_stack, bias_one.reshape(1, outs)],
        [pltpu.VMEM((3, cells, 9 * outs), jnp.float32)],
        3 * tap_flops,
        smem_first=True,
    )

    held = [(hidden[None], (0,))]
    offsets = [0]
    bit = 1
    while bit < chans:
        bit *= 2
    bit //= 2
    while bit >= 1:
        sent = jnp.stack([arr[i] for arr, offs in held for i in range(len(offs))])
        got = from_chan_partner(sent, bit)
        held.append((got, tuple(j ^ bit for j in offsets)))
        offsets = offsets + [j ^ bit for j in offsets]
        bit //= 2
    layout = tuple(offs for _, offs in held)
    me_flag = me.astype(jnp.int32).reshape(1)
    output = vmem_call(
        functools.partial(second_kernel, rows_n, cols_n, layout),
        jax.ShapeDtypeStruct((1, outs, cells), jnp.bfloat16),
        [me_flag] + [arr for arr, _ in held] + [two_stack, bias_two.reshape(1, outs)],
        [pltpu.VMEM((3, cells, count_in), jnp.bfloat16), pltpu.VMEM((1, cells, 9 * outs), jnp.float32)],
        3 * tap_flops,
        smem_first=True,
    )
    return output


def solution(mesh):
    return jax.shard_map(
        per_device,
        mesh=mesh,
        in_specs=(
            P("space", None, None, None),
            P(None, None, None, "chan", None),
            P("chan"),
            P(None, None, None, "chan", None),
            P("chan"),
        ),
        out_specs=P("space", "chan", None),
        check_vma=False,
    )
```

```python
import functools

import jax
import jax.numpy as jnp
from jax import lax
from jax.experimental import pallas as pl
from jax.experimental.pallas import tpu as pltpu
from jax.sharding import PartitionSpec as P


def gathered_from(block, source_of):
    spaces = lax.axis_size("space")
    chans = lax.axis_size("chan")
    pairs = []
    for s in range(spaces):
        for c in range(chans):
            source_s, source_c = source_of(s, c)
            pairs.append(((source_s % spaces) * chans + source_c % chans, s * chans + c))
    return lax.ppermute(block, ("space", "chan"), pairs)


def from_side(block, distance):
    return gathered_from(block, lambda s, c: (s - distance if c % 2 == 0 else s + distance, c))


def from_chan_partner(block, bit):
    return gathered_from(block, lambda s, c: (s, c ^ bit))


def spatial_sum(acc_ref, plane, rows_n, cols_n, outs):
    cells = rows_n * cols_n
    column = lax.broadcasted_iota(jnp.int32, (cells, outs), 0) % cols_n
    total = None
    for col_tap in range(3):
        shifted = None
        for row_tap in range(3):
            tap = row_tap * 3 + col_tap
            part = acc_ref[plane, :, pl.ds(tap * outs, outs)]
            amount = ((1 - row_tap) * cols_n) % cells
            if amount:
                part = pltpu.roll(part, amount, 0)
            shifted = part if shifted is None else shifted + part
        if col_tap == 0:
            shifted = jnp.where(
                column == 0,
                pltpu.roll(shifted, (1 - cols_n) % cells, 0),
                pltpu.roll(shifted, 1, 0),
            )
        elif col_tap == 2:
            shifted = jnp.where(
                column == cols_n - 1,
                pltpu.roll(shifted, cols_n - 1, 0),
                pltpu.roll(shifted, cells - 1, 0),
            )
        total = shifted if total is None else total + shifted
    return total


def tap_product(plane, w_ref, depth_tap):
    return lax.dot_general(
        plane, w_ref[depth_tap], (((1,), (1,)), ((), ())), preferred_element_type=jnp.float32
    )


def own_plane_kernel(rows_n, cols_n, x_ref, w_ref, o_ref, acc_ref):
    outs = o_ref.shape[2]
    x = x_ref[...]
    for plane in range(3):
        acc_ref[plane] = tap_product(x, w_ref, 2 - plane)
    for plane in range(3):
        o_ref[plane] = spatial_sum(acc_ref, plane, rows_n, cols_n, outs)


def side_products(acc_ref, first_ref, second_ref, w_ref, minus):
    if minus:
        acc_ref[0] = tap_product(second_ref[...], w_ref, 0)
        acc_ref[0] += tap_product(first_ref[...], w_ref, 1)
        acc_ref[1] = tap_product(first_ref[...], w_ref, 0)
        return (0, 1)
    acc_ref[1] = tap_product(first_ref[...], w_ref, 2)
    acc_ref[2] = tap_product(first_ref[...], w_ref, 1)
    acc_ref[2] += tap_product(second_ref[...], w_ref, 2)
    return (1, 2)


def fetched_side_kernel(rows_n, cols_n, odd_ref, near_ref, far_ref, w_ref, o_ref, acc_ref):
    outs = o_ref.shape[2]
    for minus in (True, False):

        @pl.when((odd_ref[0] == 0) == minus)
        def _():
            touched = side_products(acc_ref, near_ref, far_ref, w_ref, minus)
            for plane in range(3):
                if plane in touched:
                    o_ref[plane] = spatial_sum(acc_ref, plane, rows_n, cols_n, outs)
                else:
                    o_ref[plane] = jnp.zeros(o_ref.shape[1:], o_ref.dtype)


def neighbour_kernel(rows_n, cols_n, odd_ref, their_near_ref, their_far_ref, fetched_ref, part_ref,
                     w_ref, b_ref, o_ref, acc_ref):
    outs = o_ref.shape[2]
    bias = b_ref[...]
    for minus in (True, False):

        @pl.when((odd_ref[0] != 0) == minus)
        def _():
            touched = side_products(acc_ref, their_near_ref, their_far_ref, w_ref, minus)
            for plane in range(3):
                total = fetched_ref[plane] + part_ref[plane]
                if plane in touched:
                    total = total + spatial_sum(acc_ref, plane, rows_n, cols_n, outs)
                o_ref[plane] = jnp.maximum(total + bias, 0.0).astype(o_ref.dtype)


def pair_products(acc_ref, blocks, me, pairs, w_ref, field_ref, outs, first):
    width = 2 * outs
    chans = len(blocks)
    for index in range(chans):

        @pl.when(me == index)
        def _():
            started = not first
            for pair in pairs(index):
                for half in range(2):
                    ref, position = blocks[index ^ (2 * pair + half)]
                    field_ref[:, :, pl.ds(half * outs, outs)] = ref[position]
                for depth_tap in range(3):
                    term = lax.dot_general(
                        field_ref[depth_tap], w_ref[depth_tap, :, pl.ds(pair * width, width)],
                        (((1,), (1,)), ((), ())), preferred_element_type=jnp.float32,
                    )
                    if started:
                        acc_ref[0] += term
                    else:
                        acc_ref[0] = term
                        started = True


def held_blocks(inputs, layout):
    blocks = {}
    for ref, offsets in zip(inputs, layout):
        for position, j in enumerate(offsets):
            blocks[j] = (ref, position)
    return blocks


def own_pair_kernel(rows_n, cols_n, count, layout, me_ref, *refs):
    inputs = refs[:len(layout)]
    w_ref, o_ref, field_ref, acc_ref = refs[len(layout):]
    outs = o_ref.shape[2]
    me = me_ref[0]
    blocks = held_blocks(inputs, layout)
    full = {j: None for j in range(count)}
    full.update(blocks)
    pair_products(acc_ref, full, me, lambda index: [index // 2], w_ref, field_ref, outs, True)
    o_ref[0] = spatial_sum(acc_ref, 0, rows_n, cols_n, outs)


def second_kernel(rows_n, cols_n, count, layout, me_ref, *refs):
    inputs = refs[:len(layout)]
    part_ref, w_ref, b_ref, o_ref, field_ref, acc_ref = refs[len(layout):]
    outs = b_ref.shape[1]
    me = me_ref[0]
    blocks = held_blocks(inputs, layout)
    full = {j: None for j in range(count)}
    full.update(blocks)
    pairs = lambda index: [pair for pair in range(count // 2) if pair != index // 2]
    pair_products(acc_ref, full, me, pairs, w_ref, field_ref, outs, True)
    total = spatial_sum(acc_ref, 0, rows_n, cols_n, outs) + part_ref[0]
    result = jnp.maximum(total + b_ref[...], 0.0)
    o_ref[0] = result.T.astype(o_ref.dtype)


def vmem_call(kernel, out_shape, operands, scratch, flops, smem_first=False):
    specs = [pl.BlockSpec(memory_space=pltpu.VMEM) for _ in operands]
    if smem_first:
        specs[0] = pl.BlockSpec(memory_space=pltpu.SMEM)
    moved = sum(x.size * x.dtype.itemsize for x in operands) + out_shape.size * out_shape.dtype.itemsize
    return pl.pallas_call(
        kernel,
        out_shape=out_shape,
        in_specs=specs,
        out_specs=pl.BlockSpec(memory_space=pltpu.VMEM),
        scratch_shapes=scratch,
        compiler_params=pltpu.CompilerParams(vmem_limit_bytes=48 * 1024 * 1024),
        cost_estimate=pl.CostEstimate(flops=flops, transcendentals=0, bytes_accessed=moved),
    )(*operands)


def per_device(volume, weight_one, bias_one, weight_two, bias_two):
    plane = volume[0]
    rows_n, cols_n, count_in = plane.shape
    cells = rows_n * cols_n
    outs = weight_one.shape[3]
    me = lax.axis_index("chan")
    chans = lax.axis_size("chan")
    one_stack = weight_one.reshape(3, 9 * outs, count_in)
    two_stack = weight_two.reshape(3, 9 * outs, count_in)
    tap_flops = 2 * cells * count_in * 9 * outs

    flat = plane.reshape(cells, count_in)
    near, far = from_side(flat, 1), from_side(flat, 2)
    own_terms = vmem_call(
        functools.partial(own_plane_kernel, rows_n, cols_n),
        jax.ShapeDtypeStruct((3, cells, outs), jnp.float32),
        [flat, one_stack],
        [pltpu.VMEM((3, cells, 9 * outs), jnp.float32)],
        3 * tap_flops,
    )
    near, far, own_terms = lax.optimization_barrier((near, far, own_terms))
    their_near, their_far = from_chan_partner(near, 1), from_chan_partner(far, 1)
    odd = (me % 2).astype(jnp.int32).reshape(1)
    fetched_terms = vmem_call(
        functools.partial(fetched_side_kernel, rows_n, cols_n),
        jax.ShapeDtypeStruct((3, cells, outs), jnp.float32),
        [odd, near, far, one_stack],
        [pltpu.VMEM((3, cells, 9 * outs), jnp.float32)],
        3 * tap_flops,
        smem_first=True,
    )
    hidden = vmem_call(
        functools.partial(neighbour_kernel, rows_n, cols_n),
        jax.ShapeDtypeStruct((3, cells, outs), jnp.bfloat16),
        [odd, their_near, their_far, fetched_terms, own_terms, one_stack, bias_one.reshape(1, outs)],
        [pltpu.VMEM((3, cells, 9 * outs), jnp.float32)],
        3 * tap_flops,
        smem_first=True,
    )

    partner = from_chan_partner(hidden, 1)
    remote = [(hidden[None], (0,))]
    offsets = [0]
    bit = 2
    while bit < chans:
        sent = jnp.stack([arr[i] for arr, offs in remote for i in range(len(offs))])
        got = from_chan_partner(sent, bit)
        remote.append((got, tuple(j ^ bit for j in offsets)))
        offsets = offsets + [j ^ bit for j in offsets]
        bit *= 2
    me_flag = me.astype(jnp.int32).reshape(1)
    own_pair = vmem_call(
        functools.partial(own_pair_kernel, rows_n, cols_n, chans, ((0,), (1,))),
        jax.ShapeDtypeStruct((1, cells, outs), jnp.float32),
        [me_flag, hidden[None], partner[None], two_stack],
        [pltpu.VMEM((3, cells, 2 * outs), jnp.bfloat16), pltpu.VMEM((1, cells, 9 * outs), jnp.float32)],
        2 * tap_flops // chans,
        smem_first=True,
    )
    received = remote[1:]
    arrived, own_pair = lax.optimization_barrier(([arr for arr, _ in received], own_pair))
    received = [(arr, offs) for arr, (_, offs) in zip(arrived, received)]
    sent = jnp.stack([arr[i] for arr, offs in received for i in range(len(offs))])
    forwarded = from_chan_partner(sent, 1)
    held = received + [(forwarded, tuple(j ^ 1 for _, offs in received for j in offs))]
    layout = tuple(offs for _, offs in held)
    output = vmem_call(
        functools.partial(second_kernel, rows_n, cols_n, chans, layout),
        jax.ShapeDtypeStruct((1, outs, cells), jnp.bfloat16),
        [me_flag] + [arr for arr, _ in held] + [own_pair, two_stack, bias_two.reshape(1, outs)],
        [pltpu.VMEM((3, cells, 2 * outs), jnp.bfloat16), pltpu.VMEM((1, cells, 9 * outs), jnp.float32)],
        3 * tap_flops - 2 * tap_flops // chans,
        smem_first=True,
    )
    return output


def solution(mesh):
    return jax.shard_map(
        per_device,
        mesh=mesh,
        in_specs=(
            P("space", None, None, None),
            P(None, None, None, "chan", None),
            P("chan"),
            P(None, None, None, "chan", None),
            P("chan"),
        ),
        out_specs=P("space", "chan", None),
        check_vma=False,
    )
```

```python
import functools

import jax
import jax.numpy as jnp
from jax import lax
from jax.experimental import pallas as pl
from jax.experimental.pallas import tpu as pltpu
from jax.sharding import PartitionSpec as P


def gathered_from(block, source_of):
    spaces = lax.axis_size("space")
    chans = lax.axis_size("chan")
    pairs = []
    for s in range(spaces):
        for c in range(chans):
            source_s, source_c = source_of(s, c)
            pairs.append(((source_s % spaces) * chans + source_c % chans, s * chans + c))
    return lax.ppermute(block, ("space", "chan"), pairs)


def from_side(block, distance):
    return gathered_from(block, lambda s, c: (s - distance if c % 2 == 0 else s + distance, c))


def from_chan_partner(block, bit):
    return gathered_from(block, lambda s, c: (s, c ^ bit))


def spatial_sum(acc_ref, plane, rows_n, cols_n, outs):
    cells = rows_n * cols_n
    column = lax.broadcasted_iota(jnp.int32, (cells, outs), 0) % cols_n
    total = None
    for col_tap in range(3):
        shifted = None
        for row_tap in range(3):
            tap = row_tap * 3 + col_tap
            part = acc_ref[plane, :, pl.ds(tap * outs, outs)]
            amount = ((1 - row_tap) * cols_n) % cells
            if amount:
                part = pltpu.roll(part, amount, 0)
            shifted = part if shifted is None else shifted + part
        if col_tap == 0:
            shifted = jnp.where(
                column == 0,
                pltpu.roll(shifted, (1 - cols_n) % cells, 0),
                pltpu.roll(shifted, 1, 0),
            )
        elif col_tap == 2:
            shifted = jnp.where(
                column == cols_n - 1,
                pltpu.roll(shifted, cols_n - 1, 0),
                pltpu.roll(shifted, cells - 1, 0),
            )
        total = shifted if total is None else total + shifted
    return total


def tap_product(plane, w_ref, depth_tap):
    return lax.dot_general(
        plane, w_ref[depth_tap], (((1,), (1,)), ((), ())), preferred_element_type=jnp.float32
    )


def own_plane_kernel(rows_n, cols_n, x_ref, w_ref, o_ref, acc_ref):
    outs = o_ref.shape[2]
    x = x_ref[...]
    for plane in range(3):
        acc_ref[plane] = tap_product(x, w_ref, 2 - plane)
    for plane in range(3):
        o_ref[plane] = spatial_sum(acc_ref, plane, rows_n, cols_n, outs)


def side_terms(acc_ref, near_ref, far_ref, w_ref, outer_tap, rows_n, cols_n, outs):
    near = near_ref[...]
    acc_ref[0] = tap_product(near, w_ref, 1)
    acc_ref[0] += tap_product(far_ref[...], w_ref, outer_tap)
    acc_ref[1] = tap_product(near, w_ref, outer_tap)
    return [spatial_sum(acc_ref, plane, rows_n, cols_n, outs) for plane in range(2)]


def fetched_side_kernel(rows_n, cols_n, odd_ref, near_ref, far_ref, w_ref, o_ref, acc_ref):
    outs = o_ref.shape[2]
    outer_tap = 2 * odd_ref[0]
    terms = side_terms(acc_ref, near_ref, far_ref, w_ref, outer_tap, rows_n, cols_n, outs)
    for plane in range(2):
        o_ref[plane] = terms[plane]


def neighbour_kernel(rows_n, cols_n, odd_ref, their_near_ref, their_far_ref, fetched_ref, part_ref,
                     w_ref, b_ref, o_ref, acc_ref):
    outs = o_ref.shape[2]
    bias = b_ref[...]
    is_odd = odd_ref[0] != 0
    outer_tap = 2 - 2 * odd_ref[0]
    outer, centre = side_terms(acc_ref, their_near_ref, their_far_ref, w_ref, outer_tap, rows_n, cols_n, outs)
    fetched_outer = fetched_ref[0]
    planes = [
        jnp.where(is_odd, outer, fetched_outer),
        centre + fetched_ref[1],
        jnp.where(is_odd, fetched_outer, outer),
    ]
    for plane in range(3):
        total = planes[plane] + part_ref[plane]
        o_ref[plane] = jnp.maximum(total + bias, 0.0).astype(o_ref.dtype)


def pair_products(acc_ref, blocks, me, pairs, w_ref, field_ref, outs, first):
    width = 2 * outs
    chans = len(blocks)
    for index in range(chans):

        @pl.when(me == index)
        def _():
            started = not first
            for pair in pairs(index):
                for half in range(2):
                    ref, position = blocks[index ^ (2 * pair + half)]
                    field_ref[:, :, pl.ds(half * outs, outs)] = ref[position]
                for depth_tap in range(3):
                    term = lax.dot_general(
                        field_ref[depth_tap], w_ref[depth_tap, :, pl.ds(pair * width, width)],
                        (((1,), (1,)), ((), ())), preferred_element_type=jnp.float32,
                    )
                    if started:
                        acc_ref[0] += term
                    else:
                        acc_ref[0] = term
                        started = True


def held_blocks(inputs, layout):
    blocks = {}
    for ref, offsets in zip(inputs, layout):
        for position, j in enumerate(offsets):
            blocks[j] = (ref, position)
    return blocks


def own_pair_kernel(rows_n, cols_n, count, layout, me_ref, *refs):
    inputs = refs[:len(layout)]
    w_ref, o_ref, field_ref, acc_ref = refs[len(layout):]
    outs = o_ref.shape[2]
    me = me_ref[0]
    blocks = held_blocks(inputs, layout)
    full = {j: None for j in range(count)}
    full.update(blocks)
    pair_products(acc_ref, full, me, lambda index: [index // 2], w_ref, field_ref, outs, True)
    o_ref[0] = spatial_sum(acc_ref, 0, rows_n, cols_n, outs)


def second_kernel(rows_n, cols_n, count, layout, me_ref, *refs):
    inputs = refs[:len(layout)]
    part_ref, w_ref, b_ref, o_ref, field_ref, acc_ref = refs[len(layout):]
    outs = b_ref.shape[1]
    me = me_ref[0]
    blocks = held_blocks(inputs, layout)
    full = {j: None for j in range(count)}
    full.update(blocks)
    pairs = lambda index: [pair for pair in range(count // 2) if pair != index // 2]
    pair_products(acc_ref, full, me, pairs, w_ref, field_ref, outs, True)
    total = spatial_sum(acc_ref, 0, rows_n, cols_n, outs) + part_ref[0]
    result = jnp.maximum(total + b_ref[...], 0.0)
    o_ref[0] = result.T.astype(o_ref.dtype)


def vmem_call(kernel, out_shape, operands, scratch, flops, smem_first=False):
    specs = [pl.BlockSpec(memory_space=pltpu.VMEM) for _ in operands]
    if smem_first:
        specs[0] = pl.BlockSpec(memory_space=pltpu.SMEM)
    moved = sum(x.size * x.dtype.itemsize for x in operands) + out_shape.size * out_shape.dtype.itemsize
    return pl.pallas_call(
        kernel,
        out_shape=out_shape,
        in_specs=specs,
        out_specs=pl.BlockSpec(memory_space=pltpu.VMEM),
        scratch_shapes=scratch,
        compiler_params=pltpu.CompilerParams(vmem_limit_bytes=48 * 1024 * 1024),
        cost_estimate=pl.CostEstimate(flops=flops, transcendentals=0, bytes_accessed=moved),
    )(*operands)


def per_device(volume, weight_one, bias_one, weight_two, bias_two):
    plane = volume[0]
    rows_n, cols_n, count_in = plane.shape
    cells = rows_n * cols_n
    outs = weight_one.shape[3]
    me = lax.axis_index("chan")
    chans = lax.axis_size("chan")
    one_stack = weight_one.reshape(3, 9 * outs, count_in)
    two_stack = weight_two.reshape(3, 9 * outs, count_in)
    tap_flops = 2 * cells * count_in * 9 * outs

    flat = plane.reshape(cells, count_in)
    near, far = from_side(flat, 1), from_side(flat, 2)
    own_terms = vmem_call(
        functools.partial(own_plane_kernel, rows_n, cols_n),
        jax.ShapeDtypeStruct((3, cells, outs), jnp.float32),
        [flat, one_stack],
        [pltpu.VMEM((3, cells, 9 * outs), jnp.float32)],
        3 * tap_flops,
    )
    near, far, own_terms = lax.optimization_barrier((near, far, own_terms))
    their_near, their_far = from_chan_partner(near, 1), from_chan_partner(far, 1)
    odd = (me % 2).astype(jnp.int32).reshape(1)
    fetched_terms = vmem_call(
        functools.partial(fetched_side_kernel, rows_n, cols_n),
        jax.ShapeDtypeStruct((2, cells, outs), jnp.float32),
        [odd, near, far, one_stack],
        [pltpu.VMEM((2, cells, 9 * outs), jnp.float32)],
        3 * tap_flops,
        smem_first=True,
    )
    hidden = vmem_call(
        functools.partial(neighbour_kernel, rows_n, cols_n),
        jax.ShapeDtypeStruct((3, cells, outs), jnp.bfloat16),
        [odd, their_near, their_far, fetched_terms, own_terms, one_stack, bias_one.reshape(1, outs)],
        [pltpu.VMEM((2, cells, 9 * outs), jnp.float32)],
        3 * tap_flops,
        smem_first=True,
    )

    partner = from_chan_partner(hidden, 1)
    remote = [(hidden[None], (0,))]
    offsets = [0]
    bit = 2
    while bit < chans:
        sent = jnp.stack([arr[i] for arr, offs in remote for i in range(len(offs))])
        got = from_chan_partner(sent, bit)
        remote.append((got, tuple(j ^ bit for j in offsets)))
        offsets = offsets + [j ^ bit for j in offsets]
        bit *= 2
    me_flag = me.astype(jnp.int32).reshape(1)
    own_pair = vmem_call(
        functools.partial(own_pair_kernel, rows_n, cols_n, chans, ((0,), (1,))),
        jax.ShapeDtypeStruct((1, cells, outs), jnp.float32),
        [me_flag, hidden[None], partner[None], two_stack],
        [pltpu.VMEM((3, cells, 2 * outs), jnp.bfloat16), pltpu.VMEM((1, cells, 9 * outs), jnp.float32)],
        2 * tap_flops // chans,
        smem_first=True,
    )
    received = remote[1:]
    arrived, own_pair = lax.optimization_barrier(([arr for arr, _ in received], own_pair))
    received = [(arr, offs) for arr, (_, offs) in zip(arrived, received)]
    sent = jnp.stack([arr[i] for arr, offs in received for i in range(len(offs))])
    forwarded = from_chan_partner(sent, 1)
    held = received + [(forwarded, tuple(j ^ 1 for _, offs in received for j in offs))]
    layout = tuple(offs for _, offs in held)
    output = vmem_call(
        functools.partial(second_kernel, rows_n, cols_n, chans, layout),
        jax.ShapeDtypeStruct((1, outs, cells), jnp.bfloat16),
        [me_flag] + [arr for arr, _ in held] + [own_pair, two_stack, bias_two.reshape(1, outs)],
        [pltpu.VMEM((3, cells, 2 * outs), jnp.bfloat16), pltpu.VMEM((1, cells, 9 * outs), jnp.float32)],
        3 * tap_flops - 2 * tap_flops // chans,
        smem_first=True,
    )
    return output


def solution(mesh):
    return jax.shard_map(
        per_device,
        mesh=mesh,
        in_specs=(
            P("space", None, None, None),
            P(None, None, None, "chan", None),
            P("chan"),
            P(None, None, None, "chan", None),
            P("chan"),
        ),
        out_specs=P("space", "chan", None),
        check_vma=False,
    )
```

```python
import functools

import jax
import jax.numpy as jnp
from jax import lax
from jax.experimental import pallas as pl
from jax.experimental.pallas import tpu as pltpu
from jax.sharding import PartitionSpec as P


def gathered_from(block, source_of):
    spaces = lax.axis_size("space")
    chans = lax.axis_size("chan")
    pairs = []
    for s in range(spaces):
        for c in range(chans):
            source_s, source_c = source_of(s, c)
            pairs.append(((source_s % spaces) * chans + source_c % chans, s * chans + c))
    return lax.ppermute(block, ("space", "chan"), pairs)


def from_side(block, distance):
    return gathered_from(block, lambda s, c: (s - distance if c % 2 == 0 else s + distance, c))


def from_chan_partner(block, bit):
    return gathered_from(block, lambda s, c: (s, c ^ bit))


def spatial_sum(acc_ref, plane, rows_n, cols_n, outs):
    cells = rows_n * cols_n
    column = lax.broadcasted_iota(jnp.int32, (cells, outs), 0) % cols_n
    total = None
    for col_tap in range(3):
        shifted = None
        for row_tap in range(3):
            tap = row_tap * 3 + col_tap
            part = acc_ref[plane, :, pl.ds(tap * outs, outs)]
            amount = ((1 - row_tap) * cols_n) % cells
            if amount:
                part = pltpu.roll(part, amount, 0)
            shifted = part if shifted is None else shifted + part
        if col_tap == 0:
            shifted = jnp.where(
                column == 0,
                pltpu.roll(shifted, (1 - cols_n) % cells, 0),
                pltpu.roll(shifted, 1, 0),
            )
        elif col_tap == 2:
            shifted = jnp.where(
                column == cols_n - 1,
                pltpu.roll(shifted, cols_n - 1, 0),
                pltpu.roll(shifted, cells - 1, 0),
            )
        total = shifted if total is None else total + shifted
    return total


def tap_product(plane, w_ref, depth_tap):
    return lax.dot_general(
        plane, w_ref[depth_tap], (((1,), (1,)), ((), ())), preferred_element_type=jnp.float32
    )


def own_plane_kernel(rows_n, cols_n, x_ref, w_ref, o_ref, acc_ref):
    outs = o_ref.shape[2]
    x = x_ref[...]
    for plane in range(3):
        acc_ref[plane] = tap_product(x, w_ref, 2 - plane)
    for plane in range(3):
        o_ref[plane] = spatial_sum(acc_ref, plane, rows_n, cols_n, outs)


def side_products(acc_ref, first_ref, second_ref, w_ref, minus):
    if minus:
        acc_ref[0] = tap_product(second_ref[...], w_ref, 0)
        acc_ref[0] += tap_product(first_ref[...], w_ref, 1)
        acc_ref[1] = tap_product(first_ref[...], w_ref, 0)
        return (0, 1)
    acc_ref[1] = tap_product(first_ref[...], w_ref, 2)
    acc_ref[2] = tap_product(first_ref[...], w_ref, 1)
    acc_ref[2] += tap_product(second_ref[...], w_ref, 2)
    return (1, 2)


def fetched_side_kernel(rows_n, cols_n, odd_ref, near_ref, far_ref, w_ref, o_ref, acc_ref):
    outs = o_ref.shape[2]
    for minus in (True, False):

        @pl.when((odd_ref[0] == 0) == minus)
        def _():
            touched = side_products(acc_ref, near_ref, far_ref, w_ref, minus)
            for plane in range(3):
                if plane in touched:
                    o_ref[plane] = spatial_sum(acc_ref, plane, rows_n, cols_n, outs)
                else:
                    o_ref[plane] = jnp.zeros(o_ref.shape[1:], o_ref.dtype)


def neighbour_kernel(rows_n, cols_n, odd_ref, their_near_ref, their_far_ref, fetched_ref, part_ref,
                     w_ref, b_ref, o_ref, acc_ref):
    outs = o_ref.shape[2]
    bias = b_ref[...]
    for minus in (True, False):

        @pl.when((odd_ref[0] != 0) == minus)
        def _():
            touched = side_products(acc_ref, their_near_ref, their_far_ref, w_ref, minus)
            for plane in range(3):
                total = fetched_ref[plane] + part_ref[plane]
                if plane in touched:
                    total = total + spatial_sum(acc_ref, plane, rows_n, cols_n, outs)
                o_ref[plane] = jnp.maximum(total + bias, 0.0).astype(o_ref.dtype)


def pair_products(acc_ref, blocks, me, pairs, w_ref, field_ref, outs, first):
    width = 2 * outs
    chans = len(blocks)
    for index in range(chans):

        @pl.when(me == index)
        def _():
            started = not first
            for pair in pairs(index):
                for half in range(2):
                    ref, position = blocks[index ^ (2 * pair + half)]
                    field_ref[:, :, pl.ds(half * outs, outs)] = ref[position]
                for depth_tap in range(3):
                    term = lax.dot_general(
                        field_ref[depth_tap], w_ref[depth_tap, :, pl.ds(pair * width, width)],
                        (((1,), (1,)), ((), ())), preferred_element_type=jnp.float32,
                    )
                    if started:
                        acc_ref[0] += term
                    else:
                        acc_ref[0] = term
                        started = True


def held_blocks(inputs, layout):
    blocks = {}
    for ref, offsets in zip(inputs, layout):
        for position, j in enumerate(offsets):
            blocks[j] = (ref, position)
    return blocks


def own_pair_kernel(rows_n, cols_n, count, layout, me_ref, *refs):
    inputs = refs[:len(layout)]
    w_ref, o_ref, field_ref, acc_ref = refs[len(layout):]
    outs = o_ref.shape[2]
    me = me_ref[0]
    blocks = held_blocks(inputs, layout)
    full = {j: None for j in range(count)}
    full.update(blocks)
    pair_products(acc_ref, full, me, lambda index: [index // 2], w_ref, field_ref, outs, True)
    o_ref[0] = spatial_sum(acc_ref, 0, rows_n, cols_n, outs)


def second_kernel(rows_n, cols_n, count, layout, me_ref, *refs):
    inputs = refs[:len(layout)]
    part_ref, w_ref, b_ref, o_ref, field_ref, acc_ref = refs[len(layout):]
    outs = b_ref.shape[1]
    me = me_ref[0]
    blocks = held_blocks(inputs, layout)
    full = {j: None for j in range(count)}
    full.update(blocks)
    pairs = lambda index: [pair for pair in range(count // 2) if pair != index // 2]
    pair_products(acc_ref, full, me, pairs, w_ref, field_ref, outs, True)
    total = spatial_sum(acc_ref, 0, rows_n, cols_n, outs) + part_ref[0]
    result = jnp.maximum(total + b_ref[...], 0.0)
    o_ref[0] = result.astype(o_ref.dtype)


def vmem_call(kernel, out_shape, operands, scratch, flops, smem_first=False):
    specs = [pl.BlockSpec(memory_space=pltpu.VMEM) for _ in operands]
    if smem_first:
        specs[0] = pl.BlockSpec(memory_space=pltpu.SMEM)
    moved = sum(x.size * x.dtype.itemsize for x in operands) + out_shape.size * out_shape.dtype.itemsize
    return pl.pallas_call(
        kernel,
        out_shape=out_shape,
        in_specs=specs,
        out_specs=pl.BlockSpec(memory_space=pltpu.VMEM),
        scratch_shapes=scratch,
        compiler_params=pltpu.CompilerParams(vmem_limit_bytes=48 * 1024 * 1024),
        cost_estimate=pl.CostEstimate(flops=flops, transcendentals=0, bytes_accessed=moved),
    )(*operands)


def per_device(volume, weight_one, bias_one, weight_two, bias_two):
    plane = volume[0]
    rows_n, cols_n, count_in = plane.shape
    cells = rows_n * cols_n
    outs = weight_one.shape[3]
    me = lax.axis_index("chan")
    chans = lax.axis_size("chan")
    one_stack = weight_one.reshape(3, 9 * outs, count_in)
    two_stack = weight_two.reshape(3, 9 * outs, count_in)
    tap_flops = 2 * cells * count_in * 9 * outs

    flat = plane.reshape(cells, count_in)
    near, far = from_side(flat, 1), from_side(flat, 2)
    own_terms = vmem_call(
        functools.partial(own_plane_kernel, rows_n, cols_n),
        jax.ShapeDtypeStruct((3, cells, outs), jnp.float32),
        [flat, one_stack],
        [pltpu.VMEM((3, cells, 9 * outs), jnp.float32)],
        3 * tap_flops,
    )
    near, far, own_terms = lax.optimization_barrier((near, far, own_terms))
    their_near, their_far = from_chan_partner(near, 1), from_chan_partner(far, 1)
    odd = (me % 2).astype(jnp.int32).reshape(1)
    fetched_terms = vmem_call(
        functools.partial(fetched_side_kernel, rows_n, cols_n),
        jax.ShapeDtypeStruct((3, cells, outs), jnp.float32),
        [odd, near, far, one_stack],
        [pltpu.VMEM((3, cells, 9 * outs), jnp.float32)],
        3 * tap_flops,
        smem_first=True,
    )
    hidden = vmem_call(
        functools.partial(neighbour_kernel, rows_n, cols_n),
        jax.ShapeDtypeStruct((3, cells, outs), jnp.bfloat16),
        [odd, their_near, their_far, fetched_terms, own_terms, one_stack, bias_one.reshape(1, outs)],
        [pltpu.VMEM((3, cells, 9 * outs), jnp.float32)],
        3 * tap_flops,
        smem_first=True,
    )

    partner = from_chan_partner(hidden, 1)
    remote = [(hidden[None], (0,))]
    offsets = [0]
    bit = 2
    while bit < chans:
        sent = jnp.stack([arr[i] for arr, offs in remote for i in range(len(offs))])
        got = from_chan_partner(sent, bit)
        remote.append((got, tuple(j ^ bit for j in offsets)))
        offsets = offsets + [j ^ bit for j in offsets]
        bit *= 2
    me_flag = me.astype(jnp.int32).reshape(1)
    own_pair = vmem_call(
        functools.partial(own_pair_kernel, rows_n, cols_n, chans, ((0,), (1,))),
        jax.ShapeDtypeStruct((1, cells, outs), jnp.float32),
        [me_flag, hidden[None], partner[None], two_stack],
        [pltpu.VMEM((3, cells, 2 * outs), jnp.bfloat16), pltpu.VMEM((1, cells, 9 * outs), jnp.float32)],
        2 * tap_flops // chans,
        smem_first=True,
    )
    received = remote[1:]
    arrived, own_pair = lax.optimization_barrier(([arr for arr, _ in received], own_pair))
    received = [(arr, offs) for arr, (_, offs) in zip(arrived, received)]
    sent = jnp.stack([arr[i] for arr, offs in received for i in range(len(offs))])
    forwarded = from_chan_partner(sent, 1)
    held = received + [(forwarded, tuple(j ^ 1 for _, offs in received for j in offs))]
    layout = tuple(offs for _, offs in held)
    output = vmem_call(
        functools.partial(second_kernel, rows_n, cols_n, chans, layout),
        jax.ShapeDtypeStruct((1, cells, outs), jnp.bfloat16),
        [me_flag] + [arr for arr, _ in held] + [own_pair, two_stack, bias_two.reshape(1, outs)],
        [pltpu.VMEM((3, cells, 2 * outs), jnp.bfloat16), pltpu.VMEM((1, cells, 9 * outs), jnp.float32)],
        3 * tap_flops - 2 * tap_flops // chans,
        smem_first=True,
    )
    return output.transpose(0, 2, 1)


def solution(mesh):
    return jax.shard_map(
        per_device,
        mesh=mesh,
        in_specs=(
            P("space", None, None, None),
            P(None, None, None, "chan", None),
            P("chan"),
            P(None, None, None, "chan", None),
            P("chan"),
        ),
        out_specs=P("space", "chan", None),
        check_vma=False,
    )
```

```python
import functools

import jax
import jax.numpy as jnp
from jax import lax
from jax.experimental import pallas as pl
from jax.experimental.pallas import tpu as pltpu
from jax.sharding import PartitionSpec as P


def gathered_from(block, source_of):
    spaces = lax.axis_size("space")
    chans = lax.axis_size("chan")
    pairs = []
    for s in range(spaces):
        for c in range(chans):
            source_s, source_c = source_of(s, c)
            pairs.append(((source_s % spaces) * chans + source_c % chans, s * chans + c))
    return lax.ppermute(block, ("space", "chan"), pairs)


def from_side(block, distance):
    return gathered_from(block, lambda s, c: (s - distance if c % 2 == 0 else s + distance, c))


def from_chan_partner(block, bit):
    return gathered_from(block, lambda s, c: (s, c ^ bit))


def spatial_sum(acc_ref, plane, rows_n, cols_n, outs):
    cells = rows_n * cols_n
    column = lax.broadcasted_iota(jnp.int32, (cells, outs), 0) % cols_n
    total = None
    for col_tap in range(3):
        shifted = None
        for row_tap in range(3):
            tap = row_tap * 3 + col_tap
            part = acc_ref[plane, :, pl.ds(tap * outs, outs)]
            amount = ((1 - row_tap) * cols_n) % cells
            if amount:
                part = pltpu.roll(part, amount, 0)
            shifted = part if shifted is None else shifted + part
        if col_tap == 0:
            shifted = jnp.where(
                column == 0,
                pltpu.roll(shifted, (1 - cols_n) % cells, 0),
                pltpu.roll(shifted, 1, 0),
            )
        elif col_tap == 2:
            shifted = jnp.where(
                column == cols_n - 1,
                pltpu.roll(shifted, cols_n - 1, 0),
                pltpu.roll(shifted, cells - 1, 0),
            )
        total = shifted if total is None else total + shifted
    return total


def tap_product(plane, w_ref, depth_tap):
    return lax.dot_general(
        plane, w_ref[depth_tap], (((1,), (1,)), ((), ())), preferred_element_type=jnp.float32
    )


def own_plane_kernel(rows_n, cols_n, x_ref, w_ref, o_ref, acc_ref):
    outs = o_ref.shape[2]
    x = x_ref[...]
    for plane in range(3):
        acc_ref[plane] = tap_product(x, w_ref, 2 - plane)
    for plane in range(3):
        o_ref[plane] = spatial_sum(acc_ref, plane, rows_n, cols_n, outs)


def side_products(acc_ref, first_ref, second_ref, w_ref, minus):
    if minus:
        acc_ref[0] = tap_product(second_ref[...], w_ref, 0)
        acc_ref[0] += tap_product(first_ref[...], w_ref, 1)
        acc_ref[1] = tap_product(first_ref[...], w_ref, 0)
        return (0, 1)
    acc_ref[1] = tap_product(first_ref[...], w_ref, 2)
    acc_ref[2] = tap_product(first_ref[...], w_ref, 1)
    acc_ref[2] += tap_product(second_ref[...], w_ref, 2)
    return (1, 2)


def fetched_side_kernel(rows_n, cols_n, odd_ref, near_ref, far_ref, w_ref, o_ref, acc_ref):
    outs = o_ref.shape[2]
    for minus in (True, False):

        @pl.when((odd_ref[0] == 0) == minus)
        def _():
            touched = side_products(acc_ref, near_ref, far_ref, w_ref, minus)
            for plane in range(3):
                if plane in touched:
                    o_ref[plane] = spatial_sum(acc_ref, plane, rows_n, cols_n, outs)
                else:
                    o_ref[plane] = jnp.zeros(o_ref.shape[1:], o_ref.dtype)


def neighbour_kernel(rows_n, cols_n, odd_ref, their_near_ref, their_far_ref, fetched_ref, part_ref,
                     w_ref, b_ref, o_ref, acc_ref):
    outs = o_ref.shape[2]
    bias = b_ref[...]
    for minus in (True, False):

        @pl.when((odd_ref[0] != 0) == minus)
        def _():
            touched = side_products(acc_ref, their_near_ref, their_far_ref, w_ref, minus)
            for plane in range(3):
                total = fetched_ref[plane] + part_ref[plane]
                if plane in touched:
                    total = total + spatial_sum(acc_ref, plane, rows_n, cols_n, outs)
                o_ref[plane] = jnp.maximum(total + bias, 0.0).astype(o_ref.dtype)


def pair_products(acc_ref, blocks, me, pairs, w_ref, field_ref, outs, first):
    width = 2 * outs
    chans = len(blocks)
    for index in range(chans):

        @pl.when(me == index)
        def _():
            started = not first
            for pair in pairs(index):
                for half in range(2):
                    ref, position = blocks[index ^ (2 * pair + half)]
                    field_ref[:, :, pl.ds(half * outs, outs)] = ref[position]
                for depth_tap in range(3):
                    term = lax.dot_general(
                        field_ref[depth_tap], w_ref[depth_tap, :, pl.ds(pair * width, width)],
                        (((1,), (1,)), ((), ())), preferred_element_type=jnp.float32,
                    )
                    if started:
                        acc_ref[0] += term
                    else:
                        acc_ref[0] = term
                        started = True


def held_blocks(inputs, layout):
    blocks = {}
    for ref, offsets in zip(inputs, layout):
        for position, j in enumerate(offsets):
            blocks[j] = (ref, position)
    return blocks


def own_pair_kernel(rows_n, cols_n, count, layout, me_ref, *refs):
    inputs = refs[:len(layout)]
    w_ref, o_ref, field_ref, acc_ref = refs[len(layout):]
    outs = o_ref.shape[2]
    me = me_ref[0]
    blocks = held_blocks(inputs, layout)
    full = {j: None for j in range(count)}
    full.update(blocks)
    pair_products(acc_ref, full, me, lambda index: [index // 2], w_ref, field_ref, outs, True)
    o_ref[0] = spatial_sum(acc_ref, 0, rows_n, cols_n, outs)


def second_kernel(rows_n, cols_n, count, layout, me_ref, *refs):
    inputs = refs[:len(layout)]
    part_ref, w_ref, b_ref, o_ref, field_ref, acc_ref = refs[len(layout):]
    outs = b_ref.shape[1]
    me = me_ref[0]
    blocks = held_blocks(inputs, layout)
    full = {j: None for j in range(count)}
    full.update(blocks)
    pairs = lambda index: [pair for pair in range(count // 2) if pair != index // 2]
    pair_products(acc_ref, full, me, pairs, w_ref, field_ref, outs, True)
    total = spatial_sum(acc_ref, 0, rows_n, cols_n, outs) + part_ref[0]
    result = jnp.maximum(total + b_ref[...], 0.0).astype(o_ref.dtype)
    rows = lax.broadcasted_iota(jnp.int32, (outs, outs), 0)
    eye = (rows == lax.broadcasted_iota(jnp.int32, (outs, outs), 1)).astype(o_ref.dtype)
    flipped = lax.dot_general(eye, result, (((1,), (1,)), ((), ())), preferred_element_type=jnp.float32)
    o_ref[0] = flipped.astype(o_ref.dtype)


def vmem_call(kernel, out_shape, operands, scratch, flops, smem_first=False):
    specs = [pl.BlockSpec(memory_space=pltpu.VMEM) for _ in operands]
    if smem_first:
        specs[0] = pl.BlockSpec(memory_space=pltpu.SMEM)
    moved = sum(x.size * x.dtype.itemsize for x in operands) + out_shape.size * out_shape.dtype.itemsize
    return pl.pallas_call(
        kernel,
        out_shape=out_shape,
        in_specs=specs,
        out_specs=pl.BlockSpec(memory_space=pltpu.VMEM),
        scratch_shapes=scratch,
        compiler_params=pltpu.CompilerParams(vmem_limit_bytes=48 * 1024 * 1024),
        cost_estimate=pl.CostEstimate(flops=flops, transcendentals=0, bytes_accessed=moved),
    )(*operands)


def per_device(volume, weight_one, bias_one, weight_two, bias_two):
    plane = volume[0]
    rows_n, cols_n, count_in = plane.shape
    cells = rows_n * cols_n
    outs = weight_one.shape[3]
    me = lax.axis_index("chan")
    chans = lax.axis_size("chan")
    one_stack = weight_one.reshape(3, 9 * outs, count_in)
    two_stack = weight_two.reshape(3, 9 * outs, count_in)
    tap_flops = 2 * cells * count_in * 9 * outs

    flat = plane.reshape(cells, count_in)
    near, far = from_side(flat, 1), from_side(flat, 2)
    own_terms = vmem_call(
        functools.partial(own_plane_kernel, rows_n, cols_n),
        jax.ShapeDtypeStruct((3, cells, outs), jnp.float32),
        [flat, one_stack],
        [pltpu.VMEM((3, cells, 9 * outs), jnp.float32)],
        3 * tap_flops,
    )
    near, far, own_terms = lax.optimization_barrier((near, far, own_terms))
    their_near, their_far = from_chan_partner(near, 1), from_chan_partner(far, 1)
    odd = (me % 2).astype(jnp.int32).reshape(1)
    fetched_terms = vmem_call(
        functools.partial(fetched_side_kernel, rows_n, cols_n),
        jax.ShapeDtypeStruct((3, cells, outs), jnp.float32),
        [odd, near, far, one_stack],
        [pltpu.VMEM((3, cells, 9 * outs), jnp.float32)],
        3 * tap_flops,
        smem_first=True,
    )
    hidden = vmem_call(
        functools.partial(neighbour_kernel, rows_n, cols_n),
        jax.ShapeDtypeStruct((3, cells, outs), jnp.bfloat16),
        [odd, their_near, their_far, fetched_terms, own_terms, one_stack, bias_one.reshape(1, outs)],
        [pltpu.VMEM((3, cells, 9 * outs), jnp.float32)],
        3 * tap_flops,
        smem_first=True,
    )

    partner = from_chan_partner(hidden, 1)
    remote = [(hidden[None], (0,))]
    offsets = [0]
    bit = 2
    while bit < chans:
        sent = jnp.stack([arr[i] for arr, offs in remote for i in range(len(offs))])
        got = from_chan_partner(sent, bit)
        remote.append((got, tuple(j ^ bit for j in offsets)))
        offsets = offsets + [j ^ bit for j in offsets]
        bit *= 2
    me_flag = me.astype(jnp.int32).reshape(1)
    own_pair = vmem_call(
        functools.partial(own_pair_kernel, rows_n, cols_n, chans, ((0,), (1,))),
        jax.ShapeDtypeStruct((1, cells, outs), jnp.float32),
        [me_flag, hidden[None], partner[None], two_stack],
        [pltpu.VMEM((3, cells, 2 * outs), jnp.bfloat16), pltpu.VMEM((1, cells, 9 * outs), jnp.float32)],
        2 * tap_flops // chans,
        smem_first=True,
    )
    received = remote[1:]
    arrived, own_pair = lax.optimization_barrier(([arr for arr, _ in received], own_pair))
    received = [(arr, offs) for arr, (_, offs) in zip(arrived, received)]
    sent = jnp.stack([arr[i] for arr, offs in received for i in range(len(offs))])
    forwarded = from_chan_partner(sent, 1)
    held = received + [(forwarded, tuple(j ^ 1 for _, offs in received for j in offs))]
    layout = tuple(offs for _, offs in held)
    output = vmem_call(
        functools.partial(second_kernel, rows_n, cols_n, chans, layout),
        jax.ShapeDtypeStruct((1, outs, cells), jnp.bfloat16),
        [me_flag] + [arr for arr, _ in held] + [own_pair, two_stack, bias_two.reshape(1, outs)],
        [pltpu.VMEM((3, cells, 2 * outs), jnp.bfloat16), pltpu.VMEM((1, cells, 9 * outs), jnp.float32)],
        3 * tap_flops - 2 * tap_flops // chans,
        smem_first=True,
    )
    return output


def solution(mesh):
    return jax.shard_map(
        per_device,
        mesh=mesh,
        in_specs=(
            P("space", None, None, None),
            P(None, None, None, "chan", None),
            P("chan"),
            P(None, None, None, "chan", None),
            P("chan"),
        ),
        out_specs=P("space", "chan", None),
        check_vma=False,
    )
```

```python
import functools

import jax
import jax.numpy as jnp
from jax import lax
from jax.experimental import pallas as pl
from jax.experimental.pallas import tpu as pltpu
from jax.sharding import PartitionSpec as P


def gathered_from(block, source_of):
    spaces = lax.axis_size("space")
    chans = lax.axis_size("chan")
    pairs = []
    for s in range(spaces):
        for c in range(chans):
            source_s, source_c = source_of(s, c)
            pairs.append(((source_s % spaces) * chans + source_c % chans, s * chans + c))
    return lax.ppermute(block, ("space", "chan"), pairs)


def from_side(block, distance):
    return gathered_from(block, lambda s, c: (s - distance if c % 2 == 0 else s + distance, c))


def from_chan_partner(block, bit):
    return gathered_from(block, lambda s, c: (s, c ^ bit))


def spatial_sum(acc_ref, plane, rows_n, cols_n, outs):
    cells = rows_n * cols_n
    column = lax.broadcasted_iota(jnp.int32, (cells, outs), 0) % cols_n
    total = None
    for col_tap in range(3):
        shifted = None
        for row_tap in range(3):
            tap = row_tap * 3 + col_tap
            part = acc_ref[plane, :, pl.ds(tap * outs, outs)]
            amount = ((1 - row_tap) * cols_n) % cells
            if amount:
                part = pltpu.roll(part, amount, 0)
            shifted = part if shifted is None else shifted + part
        if col_tap == 0:
            shifted = jnp.where(
                column == 0,
                pltpu.roll(shifted, (1 - cols_n) % cells, 0),
                pltpu.roll(shifted, 1, 0),
            )
        elif col_tap == 2:
            shifted = jnp.where(
                column == cols_n - 1,
                pltpu.roll(shifted, cols_n - 1, 0),
                pltpu.roll(shifted, cells - 1, 0),
            )
        total = shifted if total is None else total + shifted
    return total


def spatial_sum_lanes(acc_ref, rows_n, cols_n, outs):
    cells = rows_n * cols_n
    column = lax.broadcasted_iota(jnp.int32, (outs, cells), 1) % cols_n
    total = None
    for col_tap in range(3):
        shifted = None
        for row_tap in range(3):
            tap = row_tap * 3 + col_tap
            part = acc_ref[pl.ds(tap * outs, outs), :]
            amount = ((1 - row_tap) * cols_n) % cells
            if amount:
                part = pltpu.roll(part, amount, 1)
            shifted = part if shifted is None else shifted + part
        if col_tap == 0:
            shifted = jnp.where(
                column == 0,
                pltpu.roll(shifted, (1 - cols_n) % cells, 1),
                pltpu.roll(shifted, 1, 1),
            )
        elif col_tap == 2:
            shifted = jnp.where(
                column == cols_n - 1,
                pltpu.roll(shifted, cols_n - 1, 1),
                pltpu.roll(shifted, cells - 1, 1),
            )
        total = shifted if total is None else total + shifted
    return total


def tap_product(plane, w_ref, depth_tap):
    return lax.dot_general(
        plane, w_ref[depth_tap], (((1,), (1,)), ((), ())), preferred_element_type=jnp.float32
    )


def own_plane_kernel(rows_n, cols_n, x_ref, w_ref, o_ref, acc_ref):
    outs = o_ref.shape[2]
    x = x_ref[...]
    for plane in range(3):
        acc_ref[plane] = tap_product(x, w_ref, 2 - plane)
    for plane in range(3):
        o_ref[plane] = spatial_sum(acc_ref, plane, rows_n, cols_n, outs)


def side_products(acc_ref, first_ref, second_ref, w_ref, minus):
    if minus:
        acc_ref[0] = tap_product(second_ref[...], w_ref, 0)
        acc_ref[0] += tap_product(first_ref[...], w_ref, 1)
        acc_ref[1] = tap_product(first_ref[...], w_ref, 0)
        return (0, 1)
    acc_ref[1] = tap_product(first_ref[...], w_ref, 2)
    acc_ref[2] = tap_product(first_ref[...], w_ref, 1)
    acc_ref[2] += tap_product(second_ref[...], w_ref, 2)
    return (1, 2)


def fetched_side_kernel(rows_n, cols_n, odd_ref, near_ref, far_ref, w_ref, o_ref, acc_ref):
    outs = o_ref.shape[2]
    for minus in (True, False):

        @pl.when((odd_ref[0] == 0) == minus)
        def _():
            touched = side_products(acc_ref, near_ref, far_ref, w_ref, minus)
            for plane in range(3):
                if plane in touched:
                    o_ref[plane] = spatial_sum(acc_ref, plane, rows_n, cols_n, outs)
                else:
                    o_ref[plane] = jnp.zeros(o_ref.shape[1:], o_ref.dtype)


def neighbour_kernel(rows_n, cols_n, odd_ref, their_near_ref, their_far_ref, fetched_ref, part_ref,
                     w_ref, b_ref, o_ref, acc_ref):
    outs = o_ref.shape[2]
    bias = b_ref[...]
    for minus in (True, False):

        @pl.when((odd_ref[0] != 0) == minus)
        def _():
            touched = side_products(acc_ref, their_near_ref, their_far_ref, w_ref, minus)
            for plane in range(3):
                total = fetched_ref[plane] + part_ref[plane]
                if plane in touched:
                    total = total + spatial_sum(acc_ref, plane, rows_n, cols_n, outs)
                o_ref[plane] = jnp.maximum(total + bias, 0.0).astype(o_ref.dtype)


def pair_products(acc_ref, blocks, me, pairs, w_ref, field_ref, outs, first):
    width = 2 * outs
    chans = len(blocks)
    for index in range(chans):

        @pl.when(me == index)
        def _():
            started = not first
            for pair in pairs(index):
                for half in range(2):
                    ref, position = blocks[index ^ (2 * pair + half)]
                    field_ref[:, :, pl.ds(half * outs, outs)] = ref[position]
                for depth_tap in range(3):
                    term = lax.dot_general(
                        w_ref[depth_tap, :, pl.ds(pair * width, width)], field_ref[depth_tap],
                        (((1,), (1,)), ((), ())), preferred_element_type=jnp.float32,
                    )
                    if started:
                        acc_ref[...] += term
                    else:
                        acc_ref[...] = term
                        started = True


def held_blocks(inputs, layout):
    blocks = {}
    for ref, offsets in zip(inputs, layout):
        for position, j in enumerate(offsets):
            blocks[j] = (ref, position)
    return blocks


def own_pair_kernel(rows_n, cols_n, count, layout, me_ref, *refs):
    inputs = refs[:len(layout)]
    w_ref, o_ref, field_ref, acc_ref = refs[len(layout):]
    outs = o_ref.shape[1]
    me = me_ref[0]
    blocks = held_blocks(inputs, layout)
    full = {j: None for j in range(count)}
    full.update(blocks)
    pair_products(acc_ref, full, me, lambda index: [index // 2], w_ref, field_ref, outs, True)
    o_ref[0] = spatial_sum_lanes(acc_ref, rows_n, cols_n, outs)


def second_kernel(rows_n, cols_n, count, layout, me_ref, *refs):
    inputs = refs[:len(layout)]
    part_ref, w_ref, b_ref, o_ref, field_ref, acc_ref = refs[len(layout):]
    outs = b_ref.shape[0]
    me = me_ref[0]
    blocks = held_blocks(inputs, layout)
    full = {j: None for j in range(count)}
    full.update(blocks)
    pairs = lambda index: [pair for pair in range(count // 2) if pair != index // 2]
    pair_products(acc_ref, full, me, pairs, w_ref, field_ref, outs, True)
    total = spatial_sum_lanes(acc_ref, rows_n, cols_n, outs) + part_ref[0]
    result = jnp.maximum(total + b_ref[...], 0.0)
    o_ref[0] = result.astype(o_ref.dtype)


def vmem_call(kernel, out_shape, operands, scratch, flops, smem_first=False):
    specs = [pl.BlockSpec(memory_space=pltpu.VMEM) for _ in operands]
    if smem_first:
        specs[0] = pl.BlockSpec(memory_space=pltpu.SMEM)
    moved = sum(x.size * x.dtype.itemsize for x in operands) + out_shape.size * out_shape.dtype.itemsize
    return pl.pallas_call(
        kernel,
        out_shape=out_shape,
        in_specs=specs,
        out_specs=pl.BlockSpec(memory_space=pltpu.VMEM),
        scratch_shapes=scratch,
        compiler_params=pltpu.CompilerParams(vmem_limit_bytes=48 * 1024 * 1024),
        cost_estimate=pl.CostEstimate(flops=flops, transcendentals=0, bytes_accessed=moved),
    )(*operands)


def per_device(volume, weight_one, bias_one, weight_two, bias_two):
    plane = volume[0]
    rows_n, cols_n, count_in = plane.shape
    cells = rows_n * cols_n
    outs = weight_one.shape[3]
    me = lax.axis_index("chan")
    chans = lax.axis_size("chan")
    one_stack = weight_one.reshape(3, 9 * outs, count_in)
    two_stack = weight_two.reshape(3, 9 * outs, count_in)
    tap_flops = 2 * cells * count_in * 9 * outs

    flat = plane.reshape(cells, count_in)
    near, far = from_side(flat, 1), from_side(flat, 2)
    own_terms = vmem_call(
        functools.partial(own_plane_kernel, rows_n, cols_n),
        jax.ShapeDtypeStruct((3, cells, outs), jnp.float32),
        [flat, one_stack],
        [pltpu.VMEM((3, cells, 9 * outs), jnp.float32)],
        3 * tap_flops,
    )
    near, far, own_terms = lax.optimization_barrier((near, far, own_terms))
    their_near, their_far = from_chan_partner(near, 1), from_chan_partner(far, 1)
    odd = (me % 2).astype(jnp.int32).reshape(1)
    fetched_terms = vmem_call(
        functools.partial(fetched_side_kernel, rows_n, cols_n),
        jax.ShapeDtypeStruct((3, cells, outs), jnp.float32),
        [odd, near, far, one_stack],
        [pltpu.VMEM((3, cells, 9 * outs), jnp.float32)],
        3 * tap_flops,
        smem_first=True,
    )
    hidden = vmem_call(
        functools.partial(neighbour_kernel, rows_n, cols_n),
        jax.ShapeDtypeStruct((3, cells, outs), jnp.bfloat16),
        [odd, their_near, their_far, fetched_terms, own_terms, one_stack, bias_one.reshape(1, outs)],
        [pltpu.VMEM((3, cells, 9 * outs), jnp.float32)],
        3 * tap_flops,
        smem_first=True,
    )

    partner = from_chan_partner(hidden, 1)
    remote = [(hidden[None], (0,))]
    offsets = [0]
    bit = 2
    while bit < chans:
        sent = jnp.stack([arr[i] for arr, offs in remote for i in range(len(offs))])
        got = from_chan_partner(sent, bit)
        remote.append((got, tuple(j ^ bit for j in offsets)))
        offsets = offsets + [j ^ bit for j in offsets]
        bit *= 2
    me_flag = me.astype(jnp.int32).reshape(1)
    own_pair = vmem_call(
        functools.partial(own_pair_kernel, rows_n, cols_n, chans, ((0,), (1,))),
        jax.ShapeDtypeStruct((1, outs, cells), jnp.float32),
        [me_flag, hidden[None], partner[None], two_stack],
        [pltpu.VMEM((3, cells, 2 * outs), jnp.bfloat16), pltpu.VMEM((9 * outs, cells), jnp.float32)],
        2 * tap_flops // chans,
        smem_first=True,
    )
    received = remote[1:]
    arrived, own_pair = lax.optimization_barrier(([arr for arr, _ in received], own_pair))
    received = [(arr, offs) for arr, (_, offs) in zip(arrived, received)]
    sent = jnp.stack([arr[i] for arr, offs in received for i in range(len(offs))])
    forwarded = from_chan_partner(sent, 1)
    held = received + [(forwarded, tuple(j ^ 1 for _, offs in received for j in offs))]
    layout = tuple(offs for _, offs in held)
    output = vmem_call(
        functools.partial(second_kernel, rows_n, cols_n, chans, layout),
        jax.ShapeDtypeStruct((1, outs, cells), jnp.bfloat16),
        [me_flag] + [arr for arr, _ in held] + [own_pair, two_stack, bias_two.reshape(outs, 1)],
        [pltpu.VMEM((3, cells, 2 * outs), jnp.bfloat16), pltpu.VMEM((9 * outs, cells), jnp.float32)],
        3 * tap_flops - 2 * tap_flops // chans,
        smem_first=True,
    )
    return output


def solution(mesh):
    return jax.shard_map(
        per_device,
        mesh=mesh,
        in_specs=(
            P("space", None, None, None),
            P(None, None, None, "chan", None),
            P("chan"),
            P(None, None, None, "chan", None),
            P("chan"),
        ),
        out_specs=P("space", "chan", None),
        check_vma=False,
    )
```

```python
import functools

import jax
import jax.numpy as jnp
from jax import lax
from jax.experimental import pallas as pl
from jax.experimental.pallas import tpu as pltpu
from jax.sharding import PartitionSpec as P


def gathered_from(block, source_of):
    spaces = lax.axis_size("space")
    chans = lax.axis_size("chan")
    pairs = []
    for s in range(spaces):
        for c in range(chans):
            source_s, source_c = source_of(s, c)
            pairs.append(((source_s % spaces) * chans + source_c % chans, s * chans + c))
    return lax.ppermute(block, ("space", "chan"), pairs)


def from_side(block, distance):
    return gathered_from(block, lambda s, c: (s - distance if c % 2 == 0 else s + distance, c))


def from_chan_partner(block, bit):
    return gathered_from(block, lambda s, c: (s, c ^ bit))


def spatial_sum(acc_ref, plane, rows_n, cols_n, outs):
    cells = rows_n * cols_n
    column = lax.broadcasted_iota(jnp.int32, (cells, outs), 0) % cols_n
    total = None
    for col_tap in range(3):
        shifted = None
        for row_tap in range(3):
            tap = row_tap * 3 + col_tap
            part = acc_ref[plane, :, pl.ds(tap * outs, outs)]
            amount = ((1 - row_tap) * cols_n) % cells
            if amount:
                part = pltpu.roll(part, amount, 0)
            shifted = part if shifted is None else shifted + part
        if col_tap == 0:
            shifted = jnp.where(
                column == 0,
                pltpu.roll(shifted, (1 - cols_n) % cells, 0),
                pltpu.roll(shifted, 1, 0),
            )
        elif col_tap == 2:
            shifted = jnp.where(
                column == cols_n - 1,
                pltpu.roll(shifted, cols_n - 1, 0),
                pltpu.roll(shifted, cells - 1, 0),
            )
        total = shifted if total is None else total + shifted
    return total


def tap_product(plane, w_ref, depth_tap):
    return lax.dot_general(
        plane, w_ref[depth_tap], (((1,), (1,)), ((), ())), preferred_element_type=jnp.float32
    )


def own_plane_kernel(rows_n, cols_n, x_ref, w_ref, o_ref, acc_ref):
    outs = o_ref.shape[2]
    x = x_ref[...]
    for plane in range(3):
        acc_ref[plane] = tap_product(x, w_ref, 2 - plane)
    for plane in range(3):
        o_ref[plane] = spatial_sum(acc_ref, plane, rows_n, cols_n, outs)


def side_products(acc_ref, first_ref, second_ref, w_ref, minus):
    if minus:
        acc_ref[0] = tap_product(second_ref[...], w_ref, 0)
        acc_ref[0] += tap_product(first_ref[...], w_ref, 1)
        acc_ref[1] = tap_product(first_ref[...], w_ref, 0)
        return (0, 1)
    acc_ref[1] = tap_product(first_ref[...], w_ref, 2)
    acc_ref[2] = tap_product(first_ref[...], w_ref, 1)
    acc_ref[2] += tap_product(second_ref[...], w_ref, 2)
    return (1, 2)


def fetched_side_kernel(rows_n, cols_n, odd_ref, near_ref, far_ref, w_ref, o_ref, acc_ref):
    outs = o_ref.shape[2]
    for minus in (True, False):

        @pl.when((odd_ref[0] == 0) == minus)
        def _():
            touched = side_products(acc_ref, near_ref, far_ref, w_ref, minus)
            for plane in range(3):
                if plane in touched:
                    o_ref[plane] = spatial_sum(acc_ref, plane, rows_n, cols_n, outs)
                else:
                    o_ref[plane] = jnp.zeros(o_ref.shape[1:], o_ref.dtype)


def neighbour_kernel(rows_n, cols_n, odd_ref, their_near_ref, their_far_ref, fetched_ref, part_ref,
                     w_ref, b_ref, o_ref, acc_ref):
    outs = o_ref.shape[2]
    bias = b_ref[...]
    for minus in (True, False):

        @pl.when((odd_ref[0] != 0) == minus)
        def _():
            touched = side_products(acc_ref, their_near_ref, their_far_ref, w_ref, minus)
            for plane in range(3):
                total = fetched_ref[plane] + part_ref[plane]
                if plane in touched:
                    total = total + spatial_sum(acc_ref, plane, rows_n, cols_n, outs)
                o_ref[plane] = jnp.maximum(total + bias, 0.0).astype(o_ref.dtype)


def pair_products(acc_ref, blocks, me, pairs, w_ref, field_ref, outs, first):
    width = 2 * outs
    chans = len(blocks)
    for index in range(chans):

        @pl.when(me == index)
        def _():
            started = not first
            for pair in pairs(index):
                for half in range(2):
                    ref, position = blocks[index ^ (2 * pair + half)]
                    field_ref[:, :, pl.ds(half * outs, outs)] = ref[position]
                for depth_tap in range(3):
                    term = lax.dot_general(
                        field_ref[depth_tap], w_ref[depth_tap, :, pl.ds(pair * width, width)],
                        (((1,), (1,)), ((), ())), preferred_element_type=jnp.float32,
                    )
                    if started:
                        acc_ref[0] += term
                    else:
                        acc_ref[0] = term
                        started = True


def held_blocks(inputs, layout):
    blocks = {}
    for ref, offsets in zip(inputs, layout):
        for position, j in enumerate(offsets):
            blocks[j] = (ref, position)
    return blocks


def own_pair_kernel(rows_n, cols_n, count, layout, me_ref, *refs):
    inputs = refs[:len(layout)]
    w_ref, o_ref, field_ref, acc_ref = refs[len(layout):]
    outs = o_ref.shape[2]
    me = me_ref[0]
    blocks = held_blocks(inputs, layout)
    full = {j: None for j in range(count)}
    full.update(blocks)
    pair_products(acc_ref, full, me, lambda index: [index // 2], w_ref, field_ref, outs, True)
    o_ref[0] = spatial_sum(acc_ref, 0, rows_n, cols_n, outs)


def second_kernel(rows_n, cols_n, count, layout, me_ref, *refs):
    inputs = refs[:len(layout)]
    part_ref, w_ref, b_ref, o_ref, field_ref, acc_ref = refs[len(layout):]
    outs = b_ref.shape[1]
    me = me_ref[0]
    blocks = held_blocks(inputs, layout)
    full = {j: None for j in range(count)}
    full.update(blocks)
    pairs = lambda index: [pair for pair in range(count // 2) if pair != index // 2]
    pair_products(acc_ref, full, me, pairs, w_ref, field_ref, outs, True)
    total = spatial_sum(acc_ref, 0, rows_n, cols_n, outs) + part_ref[0]
    result = jnp.maximum(total + b_ref[...], 0.0)
    o_ref[0] = result.astype(o_ref.dtype).T


def vmem_call(kernel, out_shape, operands, scratch, flops, smem_first=False):
    specs = [pl.BlockSpec(memory_space=pltpu.VMEM) for _ in operands]
    if smem_first:
        specs[0] = pl.BlockSpec(memory_space=pltpu.SMEM)
    moved = sum(x.size * x.dtype.itemsize for x in operands) + out_shape.size * out_shape.dtype.itemsize
    return pl.pallas_call(
        kernel,
        out_shape=out_shape,
        in_specs=specs,
        out_specs=pl.BlockSpec(memory_space=pltpu.VMEM),
        scratch_shapes=scratch,
        compiler_params=pltpu.CompilerParams(vmem_limit_bytes=48 * 1024 * 1024),
        cost_estimate=pl.CostEstimate(flops=flops, transcendentals=0, bytes_accessed=moved),
    )(*operands)


def per_device(volume, weight_one, bias_one, weight_two, bias_two):
    plane = volume[0]
    rows_n, cols_n, count_in = plane.shape
    cells = rows_n * cols_n
    outs = weight_one.shape[3]
    me = lax.axis_index("chan")
    chans = lax.axis_size("chan")
    one_stack = weight_one.reshape(3, 9 * outs, count_in)
    two_stack = weight_two.reshape(3, 9 * outs, count_in)
    tap_flops = 2 * cells * count_in * 9 * outs

    flat = plane.reshape(cells, count_in)
    near, far = from_side(flat, 1), from_side(flat, 2)
    own_terms = vmem_call(
        functools.partial(own_plane_kernel, rows_n, cols_n),
        jax.ShapeDtypeStruct((3, cells, outs), jnp.float32),
        [flat, one_stack],
        [pltpu.VMEM((3, cells, 9 * outs), jnp.float32)],
        3 * tap_flops,
    )
    near, far, own_terms = lax.optimization_barrier((near, far, own_terms))
    their_near, their_far = from_chan_partner(near, 1), from_chan_partner(far, 1)
    odd = (me % 2).astype(jnp.int32).reshape(1)
    fetched_terms = vmem_call(
        functools.partial(fetched_side_kernel, rows_n, cols_n),
        jax.ShapeDtypeStruct((3, cells, outs), jnp.float32),
        [odd, near, far, one_stack],
        [pltpu.VMEM((3, cells, 9 * outs), jnp.float32)],
        3 * tap_flops,
        smem_first=True,
    )
    hidden = vmem_call(
        functools.partial(neighbour_kernel, rows_n, cols_n),
        jax.ShapeDtypeStruct((3, cells, outs), jnp.bfloat16),
        [odd, their_near, their_far, fetched_terms, own_terms, one_stack, bias_one.reshape(1, outs)],
        [pltpu.VMEM((3, cells, 9 * outs), jnp.float32)],
        3 * tap_flops,
        smem_first=True,
    )

    partner = from_chan_partner(hidden, 1)
    remote = [(hidden[None], (0,))]
    offsets = [0]
    bit = 2
    while bit < chans:
        sent = jnp.stack([arr[i] for arr, offs in remote for i in range(len(offs))])
        got = from_chan_partner(sent, bit)
        remote.append((got, tuple(j ^ bit for j in offsets)))
        offsets = offsets + [j ^ bit for j in offsets]
        bit *= 2
    me_flag = me.astype(jnp.int32).reshape(1)
    own_pair = vmem_call(
        functools.partial(own_pair_kernel, rows_n, cols_n, chans, ((0,), (1,))),
        jax.ShapeDtypeStruct((1, cells, outs), jnp.float32),
        [me_flag, hidden[None], partner[None], two_stack],
        [pltpu.VMEM((3, cells, 2 * outs), jnp.bfloat16), pltpu.VMEM((1, cells, 9 * outs), jnp.float32)],
        2 * tap_flops // chans,
        smem_first=True,
    )
    received = remote[1:]
    arrived, own_pair = lax.optimization_barrier(([arr for arr, _ in received], own_pair))
    received = [(arr, offs) for arr, (_, offs) in zip(arrived, received)]
    sent = jnp.stack([arr[i] for arr, offs in received for i in range(len(offs))])
    forwarded = from_chan_partner(sent, 1)
    held = received + [(forwarded, tuple(j ^ 1 for _, offs in received for j in offs))]
    layout = tuple(offs for _, offs in held)
    output = vmem_call(
        functools.partial(second_kernel, rows_n, cols_n, chans, layout),
        jax.ShapeDtypeStruct((1, outs, cells), jnp.bfloat16),
        [me_flag] + [arr for arr, _ in held] + [own_pair, two_stack, bias_two.reshape(1, outs)],
        [pltpu.VMEM((3, cells, 2 * outs), jnp.bfloat16), pltpu.VMEM((1, cells, 9 * outs), jnp.float32)],
        3 * tap_flops - 2 * tap_flops // chans,
        smem_first=True,
    )
    return output


def solution(mesh):
    return jax.shard_map(
        per_device,
        mesh=mesh,
        in_specs=(
            P("space", None, None, None),
            P(None, None, None, "chan", None),
            P("chan"),
            P(None, None, None, "chan", None),
            P("chan"),
        ),
        out_specs=P("space", "chan", None),
        check_vma=False,
    )
```

```python
import functools

import jax
import jax.numpy as jnp
from jax import lax
from jax.experimental import pallas as pl
from jax.experimental.pallas import tpu as pltpu
from jax.sharding import PartitionSpec as P


def gathered_from(block, source_of):
    spaces = lax.axis_size("space")
    chans = lax.axis_size("chan")
    pairs = []
    for s in range(spaces):
        for c in range(chans):
            source_s, source_c = source_of(s, c)
            pairs.append(((source_s % spaces) * chans + source_c % chans, s * chans + c))
    return lax.ppermute(block, ("space", "chan"), pairs)


def from_side(block, distance):
    return gathered_from(block, lambda s, c: (s - distance if c % 2 == 0 else s + distance, c))


def from_chan_partner(block, bit):
    return gathered_from(block, lambda s, c: (s, c ^ bit))


def spatial_sum(acc_ref, plane, rows_n, cols_n, outs):
    cells = rows_n * cols_n
    column = lax.broadcasted_iota(jnp.int32, (cells, outs), 0) % cols_n
    total = None
    for col_tap in range(3):
        shifted = None
        for row_tap in range(3):
            tap = row_tap * 3 + col_tap
            part = acc_ref[plane, :, pl.ds(tap * outs, outs)]
            amount = ((1 - row_tap) * cols_n) % cells
            if amount:
                part = pltpu.roll(part, amount, 0)
            shifted = part if shifted is None else shifted + part
        if col_tap == 0:
            shifted = jnp.where(
                column == 0,
                pltpu.roll(shifted, (1 - cols_n) % cells, 0),
                pltpu.roll(shifted, 1, 0),
            )
        elif col_tap == 2:
            shifted = jnp.where(
                column == cols_n - 1,
                pltpu.roll(shifted, cols_n - 1, 0),
                pltpu.roll(shifted, cells - 1, 0),
            )
        total = shifted if total is None else total + shifted
    return total


def tap_product(plane, w_ref, depth_tap):
    return lax.dot_general(
        plane, w_ref[depth_tap], (((1,), (1,)), ((), ())), preferred_element_type=jnp.float32
    )


def own_plane_kernel(rows_n, cols_n, x_ref, w_ref, o_ref, acc_ref):
    outs = o_ref.shape[2]
    x = x_ref[...]
    for plane in range(3):
        acc_ref[plane] = tap_product(x, w_ref, 2 - plane)
    for plane in range(3):
        o_ref[plane] = spatial_sum(acc_ref, plane, rows_n, cols_n, outs)


def side_products(acc_ref, first_ref, second_ref, w_ref, minus):
    if minus:
        acc_ref[0] = tap_product(second_ref[...], w_ref, 0)
        acc_ref[0] += tap_product(first_ref[...], w_ref, 1)
        acc_ref[1] = tap_product(first_ref[...], w_ref, 0)
        return (0, 1)
    acc_ref[1] = tap_product(first_ref[...], w_ref, 2)
    acc_ref[2] = tap_product(first_ref[...], w_ref, 1)
    acc_ref[2] += tap_product(second_ref[...], w_ref, 2)
    return (1, 2)


def fetched_side_kernel(rows_n, cols_n, odd_ref, near_ref, far_ref, w_ref, o_ref, acc_ref):
    outs = o_ref.shape[2]
    for minus in (True, False):

        @pl.when((odd_ref[0] == 0) == minus)
        def _():
            touched = side_products(acc_ref, near_ref, far_ref, w_ref, minus)
            for plane in touched:
                o_ref[plane] = spatial_sum(acc_ref, plane, rows_n, cols_n, outs)


def neighbour_kernel(rows_n, cols_n, odd_ref, their_near_ref, their_far_ref, fetched_ref, part_ref,
                     w_ref, b_ref, o_ref, acc_ref):
    outs = o_ref.shape[2]
    bias = b_ref[...]
    for minus in (True, False):

        @pl.when((odd_ref[0] != 0) == minus)
        def _():
            touched = side_products(acc_ref, their_near_ref, their_far_ref, w_ref, minus)
            for plane in range(3):
                total = part_ref[plane]
                if plane not in touched or plane == 1:
                    total = total + fetched_ref[plane]
                if plane in touched:
                    total = total + spatial_sum(acc_ref, plane, rows_n, cols_n, outs)
                o_ref[plane] = jnp.maximum(total + bias, 0.0).astype(o_ref.dtype)


def pair_products(acc_ref, blocks, me, pairs, w_ref, field_ref, outs, first):
    width = 2 * outs
    chans = len(blocks)
    for index in range(chans):

        @pl.when(me == index)
        def _():
            started = not first
            for pair in pairs(index):
                for half in range(2):
                    ref, position = blocks[index ^ (2 * pair + half)]
                    field_ref[:, :, pl.ds(half * outs, outs)] = ref[position]
                for depth_tap in range(3):
                    term = lax.dot_general(
                        field_ref[depth_tap], w_ref[depth_tap, :, pl.ds(pair * width, width)],
                        (((1,), (1,)), ((), ())), preferred_element_type=jnp.float32,
                    )
                    if started:
                        acc_ref[0] += term
                    else:
                        acc_ref[0] = term
                        started = True


def held_blocks(inputs, layout):
    blocks = {}
    for ref, offsets in zip(inputs, layout):
        for position, j in enumerate(offsets):
            blocks[j] = (ref, position)
    return blocks


def own_pair_kernel(rows_n, cols_n, count, layout, me_ref, *refs):
    inputs = refs[:len(layout)]
    w_ref, o_ref, field_ref, acc_ref = refs[len(layout):]
    outs = o_ref.shape[2]
    me = me_ref[0]
    blocks = held_blocks(inputs, layout)
    full = {j: None for j in range(count)}
    full.update(blocks)
    pair_products(acc_ref, full, me, lambda index: [index // 2], w_ref, field_ref, outs, True)
    o_ref[0] = spatial_sum(acc_ref, 0, rows_n, cols_n, outs)


def second_kernel(rows_n, cols_n, count, layout, me_ref, *refs):
    inputs = refs[:len(layout)]
    part_ref, w_ref, b_ref, o_ref, field_ref, acc_ref = refs[len(layout):]
    outs = b_ref.shape[1]
    me = me_ref[0]
    blocks = held_blocks(inputs, layout)
    full = {j: None for j in range(count)}
    full.update(blocks)
    pairs = lambda index: [pair for pair in range(count // 2) if pair != index // 2]
    pair_products(acc_ref, full, me, pairs, w_ref, field_ref, outs, True)
    total = spatial_sum(acc_ref, 0, rows_n, cols_n, outs) + part_ref[0]
    result = jnp.maximum(total + b_ref[...], 0.0)
    o_ref[0] = result.T.astype(o_ref.dtype)


def vmem_call(kernel, out_shape, operands, scratch, flops, smem_first=False):
    specs = [pl.BlockSpec(memory_space=pltpu.VMEM) for _ in operands]
    if smem_first:
        specs[0] = pl.BlockSpec(memory_space=pltpu.SMEM)
    moved = sum(x.size * x.dtype.itemsize for x in operands) + out_shape.size * out_shape.dtype.itemsize
    return pl.pallas_call(
        kernel,
        out_shape=out_shape,
        in_specs=specs,
        out_specs=pl.BlockSpec(memory_space=pltpu.VMEM),
        scratch_shapes=scratch,
        compiler_params=pltpu.CompilerParams(vmem_limit_bytes=48 * 1024 * 1024),
        cost_estimate=pl.CostEstimate(flops=flops, transcendentals=0, bytes_accessed=moved),
    )(*operands)


def per_device(volume, weight_one, bias_one, weight_two, bias_two):
    plane = volume[0]
    rows_n, cols_n, count_in = plane.shape
    cells = rows_n * cols_n
    outs = weight_one.shape[3]
    me = lax.axis_index("chan")
    chans = lax.axis_size("chan")
    one_stack = weight_one.reshape(3, 9 * outs, count_in)
    two_stack = weight_two.reshape(3, 9 * outs, count_in)
    tap_flops = 2 * cells * count_in * 9 * outs

    flat = plane.reshape(cells, count_in)
    near, far = from_side(flat, 1), from_side(flat, 2)
    own_terms = vmem_call(
        functools.partial(own_plane_kernel, rows_n, cols_n),
        jax.ShapeDtypeStruct((3, cells, outs), jnp.float32),
        [flat, one_stack],
        [pltpu.VMEM((3, cells, 9 * outs), jnp.float32)],
        3 * tap_flops,
    )
    near, far, own_terms = lax.optimization_barrier((near, far, own_terms))
    their_near, their_far = from_chan_partner(near, 1), from_chan_partner(far, 1)
    odd = (me % 2).astype(jnp.int32).reshape(1)
    fetched_terms = vmem_call(
        functools.partial(fetched_side_kernel, rows_n, cols_n),
        jax.ShapeDtypeStruct((3, cells, outs), jnp.float32),
        [odd, near, far, one_stack],
        [pltpu.VMEM((3, cells, 9 * outs), jnp.float32)],
        3 * tap_flops,
        smem_first=True,
    )
    hidden = vmem_call(
        functools.partial(neighbour_kernel, rows_n, cols_n),
        jax.ShapeDtypeStruct((3, cells, outs), jnp.bfloat16),
        [odd, their_near, their_far, fetched_terms, own_terms, one_stack, bias_one.reshape(1, outs)],
        [pltpu.VMEM((3, cells, 9 * outs), jnp.float32)],
        3 * tap_flops,
        smem_first=True,
    )

    partner = from_chan_partner(hidden, 1)
    remote = [(hidden[None], (0,))]
    offsets = [0]
    bit = 2
    while bit < chans:
        sent = jnp.stack([arr[i] for arr, offs in remote for i in range(len(offs))])
        got = from_chan_partner(sent, bit)
        remote.append((got, tuple(j ^ bit for j in offsets)))
        offsets = offsets + [j ^ bit for j in offsets]
        bit *= 2
    me_flag = me.astype(jnp.int32).reshape(1)
    own_pair = vmem_call(
        functools.partial(own_pair_kernel, rows_n, cols_n, chans, ((0,), (1,))),
        jax.ShapeDtypeStruct((1, cells, outs), jnp.float32),
        [me_flag, hidden[None], partner[None], two_stack],
        [pltpu.VMEM((3, cells, 2 * outs), jnp.bfloat16), pltpu.VMEM((1, cells, 9 * outs), jnp.float32)],
        2 * tap_flops // chans,
        smem_first=True,
    )
    received = remote[1:]
    arrived, own_pair = lax.optimization_barrier(([arr for arr, _ in received], own_pair))
    received = [(arr, offs) for arr, (_, offs) in zip(arrived, received)]
    sent = jnp.stack([arr[i] for arr, offs in received for i in range(len(offs))])
    forwarded = from_chan_partner(sent, 1)
    held = received + [(forwarded, tuple(j ^ 1 for _, offs in received for j in offs))]
    layout = tuple(offs for _, offs in held)
    output = vmem_call(
        functools.partial(second_kernel, rows_n, cols_n, chans, layout),
        jax.ShapeDtypeStruct((1, outs, cells), jnp.bfloat16),
        [me_flag] + [arr for arr, _ in held] + [own_pair, two_stack, bias_two.reshape(1, outs)],
        [pltpu.VMEM((3, cells, 2 * outs), jnp.bfloat16), pltpu.VMEM((1, cells, 9 * outs), jnp.float32)],
        3 * tap_flops - 2 * tap_flops // chans,
        smem_first=True,
    )
    return output


def solution(mesh):
    return jax.shard_map(
        per_device,
        mesh=mesh,
        in_specs=(
            P("space", None, None, None),
            P(None, None, None, "chan", None),
            P("chan"),
            P(None, None, None, "chan", None),
            P("chan"),
        ),
        out_specs=P("space", "chan", None),
        check_vma=False,
    )
```

```python
import functools

import jax
import jax.numpy as jnp
from jax import lax
from jax.experimental import pallas as pl
from jax.experimental.pallas import tpu as pltpu
from jax.sharding import PartitionSpec as P


def gathered_from(block, source_of):
    spaces = lax.axis_size("space")
    chans = lax.axis_size("chan")
    pairs = []
    for s in range(spaces):
        for c in range(chans):
            source_s, source_c = source_of(s, c)
            pairs.append(((source_s % spaces) * chans + source_c % chans, s * chans + c))
    return lax.ppermute(block, ("space", "chan"), pairs)


def from_side(block, distance):
    return gathered_from(block, lambda s, c: (s - distance if c % 2 == 0 else s + distance, c))


def from_chan_partner(block, bit):
    return gathered_from(block, lambda s, c: (s, c ^ bit))


def spatial_sum(acc_ref, plane, rows_n, cols_n, outs):
    cells = rows_n * cols_n
    column = lax.broadcasted_iota(jnp.int32, (cells, outs), 0) % cols_n
    total = None
    for col_tap in range(3):
        shifted = None
        for row_tap in range(3):
            tap = row_tap * 3 + col_tap
            part = acc_ref[plane, :, pl.ds(tap * outs, outs)]
            amount = ((1 - row_tap) * cols_n) % cells
            if amount:
                part = pltpu.roll(part, amount, 0)
            shifted = part if shifted is None else shifted + part
        if col_tap == 0:
            shifted = jnp.where(
                column == 0,
                pltpu.roll(shifted, (1 - cols_n) % cells, 0),
                pltpu.roll(shifted, 1, 0),
            )
        elif col_tap == 2:
            shifted = jnp.where(
                column == cols_n - 1,
                pltpu.roll(shifted, cols_n - 1, 0),
                pltpu.roll(shifted, cells - 1, 0),
            )
        total = shifted if total is None else total + shifted
    return total


def tap_product(plane, w_ref, depth_tap):
    return lax.dot_general(
        plane, w_ref[depth_tap], (((1,), (1,)), ((), ())), preferred_element_type=jnp.float32
    )


def own_plane_kernel(rows_n, cols_n, x_ref, w_ref, o_ref, acc_ref):
    outs = o_ref.shape[2]
    x = x_ref[...]
    for plane in range(3):
        acc_ref[plane] = tap_product(x, w_ref, 2 - plane)
    for plane in range(3):
        o_ref[plane] = spatial_sum(acc_ref, plane, rows_n, cols_n, outs)


def side_products(acc_ref, first_ref, second_ref, w_ref, minus):
    if minus:
        acc_ref[0] = tap_product(second_ref[...], w_ref, 0)
        acc_ref[0] += tap_product(first_ref[...], w_ref, 1)
        acc_ref[1] = tap_product(first_ref[...], w_ref, 0)
        return (0, 1)
    acc_ref[1] = tap_product(first_ref[...], w_ref, 2)
    acc_ref[2] = tap_product(first_ref[...], w_ref, 1)
    acc_ref[2] += tap_product(second_ref[...], w_ref, 2)
    return (1, 2)


def fetched_side_kernel(rows_n, cols_n, odd_ref, near_ref, far_ref, w_ref, o_ref, acc_ref):
    outs = o_ref.shape[2]
    for minus in (True, False):

        @pl.when((odd_ref[0] == 0) == minus)
        def _():
            touched = side_products(acc_ref, near_ref, far_ref, w_ref, minus)
            for plane in range(3):
                if plane in touched:
                    o_ref[plane] = spatial_sum(acc_ref, plane, rows_n, cols_n, outs)
                else:
                    o_ref[plane] = jnp.zeros(o_ref.shape[1:], o_ref.dtype)


def neighbour_kernel(rows_n, cols_n, odd_ref, their_near_ref, their_far_ref, fetched_ref, part_ref,
                     w_ref, b_ref, o_ref, acc_ref):
    outs = o_ref.shape[2]
    bias = b_ref[...]
    for minus in (True, False):

        @pl.when((odd_ref[0] != 0) == minus)
        def _():
            touched = side_products(acc_ref, their_near_ref, their_far_ref, w_ref, minus)
            for plane in range(3):
                total = fetched_ref[plane] + part_ref[plane]
                if plane in touched:
                    total = total + spatial_sum(acc_ref, plane, rows_n, cols_n, outs)
                o_ref[plane] = jnp.maximum(total + bias, 0.0).astype(o_ref.dtype)


def pair_products(acc_ref, blocks, me, pairs, w_ref, field_ref, outs, first):
    width = 2 * outs
    chans = len(blocks)
    for index in range(chans):

        @pl.when(me == index)
        def _():
            started = not first
            for pair in pairs(index):
                for half in range(2):
                    ref, position = blocks[index ^ (2 * pair + half)]
                    field_ref[:, :, pl.ds(half * outs, outs)] = ref[position]
                for depth_tap in range(3):
                    term = lax.dot_general(
                        field_ref[depth_tap], w_ref[depth_tap, :, pl.ds(pair * width, width)],
                        (((1,), (1,)), ((), ())), preferred_element_type=jnp.float32,
                    )
                    if started:
                        acc_ref[0] += term
                    else:
                        acc_ref[0] = term
                        started = True


def held_blocks(inputs, layout):
    blocks = {}
    for ref, offsets in zip(inputs, layout):
        for position, j in enumerate(offsets):
            blocks[j] = (ref, position)
    return blocks


def own_pair_kernel(rows_n, cols_n, count, layout, me_ref, *refs):
    inputs = refs[:len(layout)]
    w_ref, b_ref, o_ref, field_ref, acc_ref = refs[len(layout):]
    outs = o_ref.shape[2]
    me = me_ref[0]
    blocks = held_blocks(inputs, layout)
    full = {j: None for j in range(count)}
    full.update(blocks)
    pair_products(acc_ref, full, me, lambda index: [index // 2], w_ref, field_ref, outs, True)
    o_ref[0] = spatial_sum(acc_ref, 0, rows_n, cols_n, outs) + b_ref[...]


def second_kernel(rows_n, cols_n, count, layout, me_ref, *refs):
    inputs = refs[:len(layout)]
    part_ref, w_ref, b_ref, o_ref, field_ref, acc_ref = refs[len(layout):]
    outs = b_ref.shape[1]
    me = me_ref[0]
    blocks = held_blocks(inputs, layout)
    full = {j: None for j in range(count)}
    full.update(blocks)
    pairs = lambda index: [pair for pair in range(count // 2) if pair != index // 2]
    pair_products(acc_ref, full, me, pairs, w_ref, field_ref, outs, True)
    total = spatial_sum(acc_ref, 0, rows_n, cols_n, outs) + part_ref[0]
    result = jnp.maximum(total, 0.0)
    o_ref[0] = result.T.astype(o_ref.dtype)


def vmem_call(kernel, out_shape, operands, scratch, flops, smem_first=False):
    specs = [pl.BlockSpec(memory_space=pltpu.VMEM) for _ in operands]
    if smem_first:
        specs[0] = pl.BlockSpec(memory_space=pltpu.SMEM)
    moved = sum(x.size * x.dtype.itemsize for x in operands) + out_shape.size * out_shape.dtype.itemsize
    return pl.pallas_call(
        kernel,
        out_shape=out_shape,
        in_specs=specs,
        out_specs=pl.BlockSpec(memory_space=pltpu.VMEM),
        scratch_shapes=scratch,
        compiler_params=pltpu.CompilerParams(vmem_limit_bytes=48 * 1024 * 1024),
        cost_estimate=pl.CostEstimate(flops=flops, transcendentals=0, bytes_accessed=moved),
    )(*operands)


def per_device(volume, weight_one, bias_one, weight_two, bias_two):
    plane = volume[0]
    rows_n, cols_n, count_in = plane.shape
    cells = rows_n * cols_n
    outs = weight_one.shape[3]
    me = lax.axis_index("chan")
    chans = lax.axis_size("chan")
    one_stack = weight_one.reshape(3, 9 * outs, count_in)
    two_stack = weight_two.reshape(3, 9 * outs, count_in)
    tap_flops = 2 * cells * count_in * 9 * outs

    flat = plane.reshape(cells, count_in)
    near, far = from_side(flat, 1), from_side(flat, 2)
    own_terms = vmem_call(
        functools.partial(own_plane_kernel, rows_n, cols_n),
        jax.ShapeDtypeStruct((3, cells, outs), jnp.float32),
        [flat, one_stack],
        [pltpu.VMEM((3, cells, 9 * outs), jnp.float32)],
        3 * tap_flops,
    )
    near, far, own_terms = lax.optimization_barrier((near, far, own_terms))
    their_near, their_far = from_chan_partner(near, 1), from_chan_partner(far, 1)
    odd = (me % 2).astype(jnp.int32).reshape(1)
    fetched_terms = vmem_call(
        functools.partial(fetched_side_kernel, rows_n, cols_n),
        jax.ShapeDtypeStruct((3, cells, outs), jnp.float32),
        [odd, near, far, one_stack],
        [pltpu.VMEM((3, cells, 9 * outs), jnp.float32)],
        3 * tap_flops,
        smem_first=True,
    )
    hidden = vmem_call(
        functools.partial(neighbour_kernel, rows_n, cols_n),
        jax.ShapeDtypeStruct((3, cells, outs), jnp.bfloat16),
        [odd, their_near, their_far, fetched_terms, own_terms, one_stack, bias_one.reshape(1, outs)],
        [pltpu.VMEM((3, cells, 9 * outs), jnp.float32)],
        3 * tap_flops,
        smem_first=True,
    )

    partner = from_chan_partner(hidden, 1)
    remote = [(hidden[None], (0,))]
    offsets = [0]
    bit = 2
    while bit < chans:
        sent = jnp.stack([arr[i] for arr, offs in remote for i in range(len(offs))])
        got = from_chan_partner(sent, bit)
        remote.append((got, tuple(j ^ bit for j in offsets)))
        offsets = offsets + [j ^ bit for j in offsets]
        bit *= 2
    me_flag = me.astype(jnp.int32).reshape(1)
    own_pair = vmem_call(
        functools.partial(own_pair_kernel, rows_n, cols_n, chans, ((0,), (1,))),
        jax.ShapeDtypeStruct((1, cells, outs), jnp.float32),
        [me_flag, hidden[None], partner[None], two_stack, bias_two.reshape(1, outs)],
        [pltpu.VMEM((3, cells, 2 * outs), jnp.bfloat16), pltpu.VMEM((1, cells, 9 * outs), jnp.float32)],
        2 * tap_flops // chans,
        smem_first=True,
    )
    received = remote[1:]
    arrived, own_pair = lax.optimization_barrier(([arr for arr, _ in received], own_pair))
    received = [(arr, offs) for arr, (_, offs) in zip(arrived, received)]
    sent = jnp.stack([arr[i] for arr, offs in received for i in range(len(offs))])
    forwarded = from_chan_partner(sent, 1)
    held = received + [(forwarded, tuple(j ^ 1 for _, offs in received for j in offs))]
    layout = tuple(offs for _, offs in held)
    output = vmem_call(
        functools.partial(second_kernel, rows_n, cols_n, chans, layout),
        jax.ShapeDtypeStruct((1, outs, cells), jnp.bfloat16),
        [me_flag] + [arr for arr, _ in held] + [own_pair, two_stack, bias_two.reshape(1, outs)],
        [pltpu.VMEM((3, cells, 2 * outs), jnp.bfloat16), pltpu.VMEM((1, cells, 9 * outs), jnp.float32)],
        3 * tap_flops - 2 * tap_flops // chans,
        smem_first=True,
    )
    return output


def solution(mesh):
    return jax.shard_map(
        per_device,
        mesh=mesh,
        in_specs=(
            P("space", None, None, None),
            P(None, None, None, "chan", None),
            P("chan"),
            P(None, None, None, "chan", None),
            P("chan"),
        ),
        out_specs=P("space", "chan", None),
        check_vma=False,
    )
```
